128 devices in a mesh: kv: 4 (over x), tok: 32 (over z, y, core).
Axes of the slice: x: 4, y: 4, z: 4, core: 2. Of those that a mesh axis runs over, the one named last changes fastest.
Arguments:
- dec_tokens: bfloat16 [512, 5120], P('tok', 'kv'), may hold values from -60 to 60
- pre_tokens: bfloat16 [8192, 5120], P('tok', 'kv'), may hold values from -60 to 60
- w_query: bfloat16 [5120, 2560], P(None, 'kv'), may hold values from -0.078125 to 0.078125
- w_keyval: bfloat16 [5120, 2, 512], P(None, None, 'kv'), may hold values from -0.078125 to 0.078125
- b_query: float32 [2560], P('kv'), may hold values from -3 to 3
- b_keyval: float32 [2, 512], P(None, 'kv'), may hold values from -3 to 3
- dec_pool: bfloat16 [2, 393216, 512], P(None, 'tok', 'kv'), may hold values from -72 to 72
- owner_slots: int32 [512], P('tok'), may hold values from 0 to 511, each once
- dec_lengths: int32 [512], P('tok'), may hold values from 1 to 4096, as said below
- pre_cache: bfloat16 [2, 32768, 512], P(None, 'tok', 'kv'), may hold values from -72 to 72
- pre_offsets: int32 [16], replicated, may hold values from 1536 to 2048
Outputs:
- dec_attn: bfloat16 [512, 2560], P('tok', 'kv')
- pre_attn: bfloat16 [8192, 2560], P('tok', 'kv')
- new_pool: bfloat16 [2, 393216, 512], P(None, 'tok', 'kv')
- pre_keyval: bfloat16 [2, 8192, 512], P(None, 'tok', 'kv')
The draws below stay inside these ranges and needn't reach their ends.
Inputs may be any that keep to these rules, and one draw needn't show every extreme that they name: `dec_lengths`: in the 16 slots of each owner, one length is 512 or more and the others are below 512, so an owner's lengths plus one each sum to at most 12288.
All inputs are finite; a program needn't handle non-finite values.
Results may differ from the reference program's by a relative error of at most 0.0065.
The reference program's roundings to bfloat16 on the way count: a program that leaves them out, or rounds other values in their place, can miss the bound.
Values may be sent and summed in bfloat16 or wider, within the bound.
No kernel may reach another device: no remote copies, remote signals or barrier semaphores. Data moves between devices by JAX's collectives and lax.ppermute only.
A program may use at most 128 MiB of HBM per device.

```python
import jax
import jax.numpy as jnp
from jax import lax

D = 5120
HD = 128
QH = 20
KVH = 4
BLOCK = 512
PSH = 1024
LMAX = 4096
SHORT = 512
DEC_DEV = 16
DEC = 512
PRE = 16
DPOOL = 12288
N_TOK = 32


def token_rows(key, amount):
    first_key = jax.random.fold_in(key, 0)
    values = jax.random.truncated_normal(first_key, -6.0, 6.0, (amount, D), jnp.float32)
    return values.astype(jnp.bfloat16)


def cache_rows(key, length):
    first_key = jax.random.fold_in(key, 0)
    values = jax.random.truncated_normal(first_key, -6.0, 6.0, (2, length, KVH * HD), jnp.float32)
    return values.astype(jnp.bfloat16)


def draw_dec_tokens(key, part):
    return token_rows(key, DEC)


def draw_pre_tokens(key, part):
    return token_rows(key, PRE * BLOCK)


def draw_dec_pool(key, part):
    return cache_rows(key, DEC // DEC_DEV * DPOOL)


def draw_pre_cache(key, part):
    return cache_rows(key, PRE * 2 * PSH)


def draw_dec_lengths(key, part):
    keys_list = jax.random.split(key, 5)
    owner_count = DEC // DEC_DEV
    ceilings = jax.random.randint(keys_list[0], (owner_count, DEC_DEV), 2, SHORT + 1)
    short_len = jax.random.randint(keys_list[1], (owner_count, DEC_DEV), 1, ceilings)
    long_len = jax.random.randint(keys_list[2], (owner_count, 1), SHORT, LMAX + 1)
    picked = jax.random.randint(keys_list[3], (), 0, owner_count)
    long_len = jnp.where(jnp.arange(owner_count)[:, None] == picked, LMAX, long_len)
    long_slot = jax.random.randint(keys_list[4], (owner_count, 1), 0, DEC_DEV)
    lengths = jnp.where(jnp.arange(DEC_DEV)[None, :] == long_slot, long_len, short_len)
    return lengths.reshape(DEC).astype(jnp.int32)


def draw_pre_offsets(key, part):
    first_key, second_key = jax.random.split(key)
    offsets = jax.random.randint(first_key, (PRE,), PSH + PSH // 2, 2 * PSH + 1)
    picked = jax.random.randint(second_key, (), 0, PRE)
    return jnp.where(jnp.arange(PRE) == picked, 2 * PSH, offsets).astype(jnp.int32)


def level_of(own_key, extent, cuts, smallest, top_value):
    factor_of = 1.0
    for dim, blocks in cuts:
        heights = jax.random.uniform(jax.random.fold_in(jax.random.fold_in(own_key, 6), dim), (blocks,), jnp.float32, smallest / len(cuts), top_value / len(cuts))
        factor_of = factor_of * jnp.repeat(jnp.exp(heights), extent[dim] // blocks).reshape((-1,) + (1,) * (len(extent) - 1 - dim))
    return factor_of


def noise(key, extent, scale, limit, cuts=(), held_as=jnp.bfloat16):
    drawn = scale * jax.random.normal(key, extent, jnp.float32)
    if cuts:
        drawn = drawn * level_of(key, extent, cuts, -0.22, 0.18)
    return jnp.clip(drawn, -limit, limit).astype(held_as)


def setup_inputs(seed: int = 0) -> dict:
    key_of = jax.random.split(jax.random.key(seed), 12)
    return {
        "dec_tokens": draw_dec_tokens(jax.random.fold_in(key_of[11], 71), 0),
        "pre_tokens": draw_pre_tokens(jax.random.fold_in(key_of[11], 71), 0),
        "w_query": noise(key_of[2], (D, QH * HD), D ** -0.5, 0.078125, ((1, 4),)),
        "w_keyval": noise(key_of[3], (D, 2, KVH * HD), D ** -0.5, 0.078125, ((2, 4),)),
        "b_query": noise(key_of[4], (QH * HD,), 0.5, 3.0, ((0, 4),), jnp.float32),
        "b_keyval": noise(key_of[5], (2, KVH * HD), 0.5, 3.0, ((1, 4),), jnp.float32),
        "dec_pool": draw_dec_pool(jax.random.fold_in(key_of[11], 71), 0),
        "owner_slots": jax.random.permutation(key_of[7], DEC).astype(jnp.int32),
        "dec_lengths": draw_dec_lengths(jax.random.fold_in(key_of[11], 71), 0),
        "pre_cache": draw_pre_cache(jax.random.fold_in(key_of[11], 71), 0),
        "pre_offsets": draw_pre_offsets(jax.random.fold_in(key_of[11], 71), 0),
    }


THETA = 1000000.0


def rotate(values, positions):
    halfway = values.shape[-1] // 2
    spread = jnp.arange(halfway, dtype=jnp.float32) * (2.0 / values.shape[-1])
    rates = jnp.power(jnp.float32(THETA), -spread)
    angles = positions.astype(jnp.float32)[:, None] * rates[None, :]
    cosine = jnp.cos(angles)[:, None, :]
    sine = jnp.sin(angles)[:, None, :]
    former = values[..., :halfway]
    latter = values[..., halfway:]
    return jnp.concatenate([former * cosine - latter * sine, latter * cosine + former * sine], axis=-1)


def head_scores(queries, key_rows, allowed):
    amount = queries.shape[0]
    q_heads = queries.shape[1] // HD
    kv_heads = key_rows.shape[1] // HD
    per_group = q_heads // kv_heads
    shaped = queries.reshape(amount, q_heads, HD).astype(jnp.float32)
    pieces = []
    for kv_head in range(kv_heads):
        product = jnp.einsum("ngd,md->ngm", shaped[:, kv_head * per_group:(kv_head + 1) * per_group],
                             key_rows[:, kv_head * HD:(kv_head + 1) * HD].astype(jnp.float32))
        pieces.append(product)
    scores = jnp.concatenate(pieces, axis=1) * (HD ** -0.5)
    return jnp.where(allowed[:, None, :], scores, -jnp.inf)


def head_mix(scores, peaks, value_rows):
    powers = jnp.exp(scores - peaks[..., None])
    totals = jnp.sum(powers, axis=-1)
    weights = powers.astype(jnp.bfloat16)
    kv_heads = value_rows.shape[1] // HD
    per_group = scores.shape[1] // kv_heads
    pieces = []
    for kv_head in range(kv_heads):
        product = jnp.einsum("ngm,md->ngd", weights[:, kv_head * per_group:(kv_head + 1) * per_group].astype(jnp.float32),
                             value_rows[:, kv_head * HD:(kv_head + 1) * HD].astype(jnp.float32))
        pieces.append(product)
    return totals, jnp.concatenate(pieces, axis=1)


def serve_owner(queries, keyval, lengths, cache_pool):
    amount = queries.shape[0]
    q_heads = queries.shape[1] // HD
    kv_heads = cache_pool.shape[2] // HD
    finish = jnp.cumsum(lengths + 1).astype(jnp.int32)
    starts = (finish - lengths - 1).astype(jnp.int32)
    turned = rotate(queries.astype(jnp.float32).reshape(amount, q_heads, HD), lengths)
    turned = turned.astype(jnp.bfloat16).reshape(amount, q_heads * HD)
    new_keys = rotate(keyval[:, 0].astype(jnp.float32).reshape(amount, kv_heads, HD), lengths)
    new_keys = new_keys.astype(jnp.bfloat16).reshape(amount, kv_heads * HD)
    appended = jnp.stack([new_keys, keyval[:, 1]], axis=0)
    cache_pool = cache_pool.at[:, starts + lengths].set(appended)
    spots = jnp.arange(cache_pool.shape[1], dtype=jnp.int32)
    allowed = (spots[None, :] >= starts[:, None]) & (spots[None, :] <= (starts + lengths)[:, None])
    scores = head_scores(turned, cache_pool[0], allowed)
    totals, mixed = head_mix(scores, jnp.max(scores, axis=-1), cache_pool[1])
    result = (mixed / totals[..., None]).astype(jnp.bfloat16).reshape(amount, q_heads * HD)
    return result, cache_pool


def reference(dec_tokens, pre_tokens, w_query, w_keyval, b_query, b_keyval, dec_pool, owner_slots, dec_lengths, pre_cache, pre_offsets):
    width = w_keyval.shape[2]
    kv_weight = w_keyval.reshape(w_keyval.shape[0], 2 * width)
    kv_bias = b_keyval.reshape(2 * width)
    dec_query = (jnp.dot(dec_tokens, w_query, preferred_element_type=jnp.float32) + b_query).astype(jnp.bfloat16)
    dec_keyval = (jnp.dot(dec_tokens, kv_weight, preferred_element_type=jnp.float32) + kv_bias).astype(jnp.bfloat16)
    dec_query = lax.optimization_barrier(dec_query)
    dec_keyval = lax.optimization_barrier(dec_keyval).reshape(DEC, 2, width)

    def serve(owner_id):
        chosen = lax.dynamic_slice_in_dim(owner_slots, owner_id * DEC_DEV, DEC_DEV)
        lengths = lax.dynamic_slice_in_dim(dec_lengths, owner_id * DEC_DEV, DEC_DEV)
        cache_pool = lax.dynamic_slice_in_dim(dec_pool, owner_id * DPOOL, DPOOL, axis=1)
        return serve_owner(jnp.take(dec_query, chosen, axis=0), jnp.take(dec_keyval, chosen, axis=0), lengths, cache_pool)

    results, new_pools = lax.map(serve, jnp.arange(N_TOK, dtype=jnp.int32))
    dec_attn = jnp.zeros((DEC, QH * HD), jnp.bfloat16).at[owner_slots].set(results.reshape(DEC, QH * HD))
    new_pool = jnp.transpose(new_pools, (1, 0, 2, 3)).reshape(2, N_TOK * DPOOL, width)

    pre_query = jnp.dot(pre_tokens, w_query, preferred_element_type=jnp.float32) + b_query
    pre_kv = (jnp.dot(pre_tokens, kv_weight, preferred_element_type=jnp.float32) + kv_bias).reshape(PRE * BLOCK, 2, width)

    def prefill(prefill_id):
        offset = pre_offsets[prefill_id]
        positions = offset + jnp.arange(BLOCK, dtype=jnp.int32)
        queries = lax.dynamic_slice_in_dim(pre_query, prefill_id * BLOCK, BLOCK)
        keyval = lax.dynamic_slice_in_dim(pre_kv, prefill_id * BLOCK, BLOCK)
        turned = rotate(queries.reshape(BLOCK, QH, HD), positions).astype(jnp.bfloat16).reshape(BLOCK, QH * HD)
        new_keys = rotate(keyval[:, 0].reshape(BLOCK, KVH, HD), positions).astype(jnp.bfloat16).reshape(BLOCK, width)
        appended = jnp.stack([new_keys, keyval[:, 1].astype(jnp.bfloat16)], axis=0)
        history = lax.dynamic_slice_in_dim(pre_cache, prefill_id * 2 * PSH, 2 * PSH, axis=1)
        key_rows = jnp.concatenate([history, appended], axis=1)
        key_slots = jnp.arange(2 * PSH + BLOCK, dtype=jnp.int32)
        key_pos = jnp.where(key_slots < 2 * PSH, key_slots, offset + key_slots - 2 * PSH)
        usable = (key_slots < offset) | (key_slots >= 2 * PSH)
        allowed = usable[None, :] & (key_pos[None, :] <= positions[:, None])
        scores = head_scores(turned, key_rows[0], allowed)
        totals, mixed = head_mix(scores, jnp.max(scores, axis=-1), key_rows[1])
        return (mixed / totals[..., None]).astype(jnp.bfloat16).reshape(BLOCK, QH * HD), appended

    pre_results, pre_new = lax.map(prefill, jnp.arange(PRE, dtype=jnp.int32))
    pre_attn = pre_results.reshape(PRE * BLOCK, QH * HD)
    pre_keyval = jnp.transpose(pre_new, (1, 0, 2, 3)).reshape(2, PRE * BLOCK, width)
    return dec_attn, pre_attn, new_pool, pre_keyval
```

```python
import jax
import jax.numpy as jnp
from jax import lax
from jax.sharding import PartitionSpec as P

HD = 128


THETA = 1000000.0


def swapped(value, axis, distance):
    return lax.ppermute(value, axis, [(i, i ^ 1 << distance) for i in range(lax.axis_size(axis))])


def rotate(values, positions):
    halfway = values.shape[-1] // 2
    spread = jnp.arange(halfway, dtype=jnp.float32) * (2.0 / values.shape[-1])
    rates = jnp.power(jnp.float32(THETA), -spread)
    angles = positions.astype(jnp.float32)[:, None] * rates[None, :]
    cosine = jnp.cos(angles)[:, None, :]
    sine = jnp.sin(angles)[:, None, :]
    former = values[..., :halfway]
    latter = values[..., halfway:]
    return jnp.concatenate(
        [former * cosine - latter * sine, latter * cosine + former * sine], axis=-1
    )


def head_scores(queries, key_rows, allowed):
    amount = queries.shape[0]
    q_heads = queries.shape[1] // HD
    shaped = queries.reshape(amount, q_heads, HD)
    product = jnp.einsum("ngd,md->ngm", shaped, key_rows, preferred_element_type=jnp.float32)
    scores = product * HD ** (-0.5)
    return jnp.where(allowed[:, None, :], scores, -jnp.inf)


def head_mix(scores, peaks, value_rows):
    powers = jnp.exp(scores - peaks[..., None])
    totals = jnp.sum(powers, axis=-1)
    weights = powers.astype(jnp.bfloat16)
    product = jnp.einsum("ngm,md->ngd", weights, value_rows, preferred_element_type=jnp.float32)
    return (totals, product)


def serve_owner(queries, keyval, lengths, cache_pool):
    amount = queries.shape[0]
    q_heads = queries.shape[1] // HD
    kv_heads = cache_pool.shape[2] // HD
    finish = jnp.cumsum(lengths + 1)
    starts = finish - lengths - 1
    turned = rotate(queries.astype(jnp.float32).reshape(amount, q_heads, HD), lengths)
    turned = turned.astype(jnp.bfloat16).reshape(amount, q_heads * HD)
    new_keys = rotate(keyval[:, 0].astype(jnp.float32).reshape(amount, kv_heads, HD), lengths)
    new_keys = new_keys.astype(jnp.bfloat16).reshape(amount, kv_heads * HD)
    appended = jnp.stack([new_keys, keyval[:, 1]], axis=0)
    cache_pool = cache_pool.at[:, starts + lengths].set(appended)
    spots = jnp.arange(cache_pool.shape[1], dtype=jnp.int32)
    allowed = (spots[None, :] >= starts[:, None]) & (spots[None, :] <= (starts + lengths)[:, None])
    scores = head_scores(turned, cache_pool[0], allowed)
    totals, mixed = head_mix(scores, jnp.max(scores, axis=-1), cache_pool[1])
    result = (mixed / totals[..., None]).astype(jnp.bfloat16).reshape(amount, q_heads * HD)
    return (result, cache_pool)


def fan(value, axis):
    count = lax.axis_size(axis)
    parts = [value]
    for shift in range(1, count):
        parts.append(lax.ppermute(value, axis, [(i, (i + shift) % count) for i in range(count)]))
    return parts


def project(rows, weight, bias):
    parts = fan(rows, "kv")
    place = lax.axis_index("kv")
    width = rows.shape[1]
    total = None
    for shift, part in enumerate(parts):
        source = (place - shift) % len(parts)
        block = lax.dynamic_slice_in_dim(weight, source * width, width, axis=0)
        piece = jnp.dot(part, block, preferred_element_type=jnp.float32)
        total = piece if total is None else total + piece
    return total + bias


def body(
    dec_tokens,
    pre_tokens,
    w_query,
    w_keyval,
    b_query,
    b_keyval,
    dec_pool,
    owner_slots,
    dec_lengths,
    pre_cache,
    pre_offsets,
):
    dec_count = dec_tokens.shape[0]
    pre_count = pre_tokens.shape[0]
    q_width = w_query.shape[1]
    kv_width = w_keyval.shape[2]
    kv_weight = w_keyval.reshape(w_keyval.shape[0], 2 * kv_width)
    weight = jnp.concatenate([w_query, kv_weight], axis=1)
    bias = jnp.concatenate([b_query, b_keyval.reshape(2 * kv_width)])
    dec_all = project(dec_tokens, weight, bias).astype(jnp.bfloat16)
    tok_count = lax.axis_size("tok")
    tok_place = lax.axis_index("tok")
    ids = jnp.stack([owner_slots // dec_count, owner_slots % dec_count], axis=1).astype(jnp.bfloat16)
    send_width = -(-(q_width + 2 * kv_width + 2) // 128) * 128
    pad = jnp.zeros((dec_count, send_width - q_width - 2 * kv_width - 2), jnp.bfloat16)
    sent = jnp.concatenate([dec_all, ids, pad], axis=1)
    got = jnp.concatenate(fan(sent, "tok"), axis=0)
    source = owner_slots // dec_count
    rows = ((tok_place - source) % tok_count) * dec_count + owner_slots % dec_count
    chosen = jnp.take(got, rows, axis=0)
    dec_query = chosen[:, :q_width]
    dec_keyval = chosen[:, q_width:q_width + 2 * kv_width].reshape(dec_count, 2, kv_width)
    served, new_pool = serve_owner(dec_query, dec_keyval, dec_lengths, dec_pool)
    back = jnp.concatenate(fan(served, "tok"), axis=0)
    got_ids = got[:, q_width + 2 * kv_width:q_width + 2 * kv_width + 2].astype(jnp.int32)
    requests = got_ids[:, 0] * dec_count + got_ids[:, 1]
    wanted = tok_place * dec_count + jnp.arange(dec_count, dtype=jnp.int32)
    where = jnp.argmax(requests[None, :] == wanted[:, None], axis=1)
    dec_attn = jnp.take(back, where, axis=0)
    pre_all = project(pre_tokens, weight, bias)
    all_query = pre_all[:, :q_width]
    all_keyval = pre_all[:, q_width:]
    half_id = tok_place % 2
    offset = pre_offsets[tok_place // 2]
    local_pos = jnp.arange(pre_count, dtype=jnp.int32)
    positions = offset + half_id * pre_count + local_pos
    q_heads = q_width // HD
    kv_heads = kv_width // HD
    turned = rotate(all_query.reshape(pre_count, q_heads, HD), positions)
    turned = turned.astype(jnp.bfloat16).reshape(pre_count, q_width)
    pre_kv = all_keyval.reshape(pre_count, 2, kv_width)
    new_keys = rotate(pre_kv[:, 0].reshape(pre_count, kv_heads, HD), positions)
    new_keys = new_keys.astype(jnp.bfloat16).reshape(pre_count, kv_width)
    appended = jnp.stack([new_keys, pre_kv[:, 1].astype(jnp.bfloat16)], axis=0)
    shard = pre_cache.shape[1]
    other_cache, other_new = swapped((pre_cache, appended), "tok", 0)
    is_lower = half_id == 0
    history = jnp.where(
        is_lower,
        jnp.concatenate([pre_cache, other_cache], axis=1),
        jnp.concatenate([other_cache, pre_cache], axis=1),
    )
    block_rows = jnp.where(
        is_lower,
        jnp.concatenate([appended, other_new], axis=1),
        jnp.concatenate([other_new, appended], axis=1),
    )
    key_rows = jnp.concatenate([history, block_rows], axis=1)
    key_slots = jnp.arange(key_rows.shape[1], dtype=jnp.int32)
    key_pos = jnp.where(key_slots < 2 * shard, key_slots, offset + key_slots - 2 * shard)
    usable = (key_slots < offset) | (key_slots >= 2 * shard)
    allowed = usable[None, :] & (key_pos[None, :] <= positions[:, None])
    scores = head_scores(turned, key_rows[0], allowed)
    totals, mixed = head_mix(scores, jnp.max(scores, axis=-1), key_rows[1])
    pre_attn = (mixed / totals[..., None]).astype(jnp.bfloat16).reshape(pre_count, q_width)
    return (dec_attn, pre_attn, new_pool, appended)


def solution(mesh):
    in_specs = (
        P("tok", "kv"),
        P("tok", "kv"),
        P(None, "kv"),
        P(None, None, "kv"),
        P("kv"),
        P(None, "kv"),
        P(None, "tok", "kv"),
        P("tok"),
        P("tok"),
        P(None, "tok", "kv"),
        P(),
    )
    out_specs = (P("tok", "kv"), P("tok", "kv"), P(None, "tok", "kv"), P(None, "tok", "kv"))
    return jax.shard_map(body, mesh=mesh, in_specs=in_specs, out_specs=out_specs, check_vma=False)
```

```python
import jax
import jax.numpy as jnp
from jax import lax
from jax.sharding import PartitionSpec as P

HD = 128


THETA = 1000000.0


def swapped(value, axis, distance):
    return lax.ppermute(value, axis, [(i, i ^ 1 << distance) for i in range(lax.axis_size(axis))])


def rotate(values, positions):
    halfway = values.shape[-1] // 2
    spread = jnp.arange(halfway, dtype=jnp.float32) * (2.0 / values.shape[-1])
    rates = jnp.power(jnp.float32(THETA), -spread)
    angles = positions.astype(jnp.float32)[:, None] * rates[None, :]
    cosine = jnp.cos(angles)[:, None, :]
    sine = jnp.sin(angles)[:, None, :]
    former = values[..., :halfway]
    latter = values[..., halfway:]
    return jnp.concatenate(
        [former * cosine - latter * sine, latter * cosine + former * sine], axis=-1
    )


def head_scores(queries, key_rows, allowed):
    amount = queries.shape[0]
    q_heads = queries.shape[1] // HD
    shaped = queries.reshape(amount, q_heads, HD)
    product = jnp.einsum("ngd,md->ngm", shaped, key_rows, preferred_element_type=jnp.float32)
    scores = product * HD ** (-0.5)
    return jnp.where(allowed[:, None, :], scores, -jnp.inf)


def head_mix(scores, peaks, value_rows):
    powers = jnp.exp(scores - peaks[..., None])
    totals = jnp.sum(powers, axis=-1)
    weights = powers.astype(jnp.bfloat16)
    product = jnp.einsum("ngm,md->ngd", weights, value_rows, preferred_element_type=jnp.float32)
    return (totals, product)


def serve_owner(queries, keyval, lengths, cache_pool):
    amount = queries.shape[0]
    q_heads = queries.shape[1] // HD
    kv_heads = cache_pool.shape[2] // HD
    finish = jnp.cumsum(lengths + 1)
    starts = finish - lengths - 1
    turned = rotate(queries.astype(jnp.float32).reshape(amount, q_heads, HD), lengths)
    turned = turned.astype(jnp.bfloat16).reshape(amount, q_heads * HD)
    new_keys = rotate(keyval[:, 0].astype(jnp.float32).reshape(amount, kv_heads, HD), lengths)
    new_keys = new_keys.astype(jnp.bfloat16).reshape(amount, kv_heads * HD)
    appended = jnp.stack([new_keys, keyval[:, 1]], axis=0)
    cache_pool = cache_pool.at[:, starts + lengths].set(appended)
    spots = jnp.arange(cache_pool.shape[1], dtype=jnp.int32)
    allowed = (spots[None, :] >= starts[:, None]) & (spots[None, :] <= (starts + lengths)[:, None])
    scores = head_scores(turned, cache_pool[0], allowed)
    totals, mixed = head_mix(scores, jnp.max(scores, axis=-1), cache_pool[1])
    result = (mixed / totals[..., None]).astype(jnp.bfloat16).reshape(amount, q_heads * HD)
    return (result, cache_pool)


def tree_gather(value):
    place = lax.axis_index("tok")
    buffer = value
    for stride, count in ((1, 2), (2, 4), (8, 4)):
        parts = [buffer]
        for shift in range(1, count):
            pairs = []
            for i in range(32):
                digit = (i // stride) % count
                target = i + (((digit + shift) % count) - digit) * stride
                pairs.append((i, target))
            parts.append(lax.ppermute(buffer, "tok", pairs))
        buffer = jnp.concatenate(parts, axis=0)
    return buffer


def tree_row(place, source, rows):
    core = (place % 2) ^ (source % 2)
    y = ((place // 2) % 4 - (source // 2) % 4) % 4
    z = (place // 8 - source // 8) % 4
    return ((z * 4 + y) * 2 + core) * rows


def project(rows, w_query, kv_weight, b_query, kv_bias):
    cols = lax.all_gather(rows, "kv", axis=1, tiled=True)
    query = jnp.dot(cols, w_query, preferred_element_type=jnp.float32) + b_query
    keyval = jnp.dot(cols, kv_weight, preferred_element_type=jnp.float32) + kv_bias
    return query, keyval


def body(
    dec_tokens,
    pre_tokens,
    w_query,
    w_keyval,
    b_query,
    b_keyval,
    dec_pool,
    owner_slots,
    dec_lengths,
    pre_cache,
    pre_offsets,
):
    dec_count = dec_tokens.shape[0]
    pre_count = pre_tokens.shape[0]
    q_width = w_query.shape[1]
    kv_width = w_keyval.shape[2]
    kv_weight = w_keyval.reshape(w_keyval.shape[0], 2 * kv_width)
    kv_bias = b_keyval.reshape(2 * kv_width)
    dec_q, dec_kv = project(dec_tokens, w_query, kv_weight, b_query, kv_bias)
    tok_place = lax.axis_index("tok")
    ids = jnp.stack([owner_slots // dec_count, owner_slots % dec_count], axis=1).astype(jnp.bfloat16)
    used = q_width + 2 * kv_width + 2
    pad = jnp.zeros((dec_count, -(-used // 128) * 128 - used), jnp.bfloat16)
    sent = jnp.concatenate([dec_q.astype(jnp.bfloat16), dec_kv.astype(jnp.bfloat16), ids, pad], axis=1)
    got = tree_gather(sent)
    rows = tree_row(tok_place, owner_slots // dec_count, dec_count) + owner_slots % dec_count
    chosen = jnp.take(got, rows, axis=0)
    dec_query = chosen[:, :q_width]
    dec_keyval = chosen[:, q_width:q_width + 2 * kv_width].reshape(dec_count, 2, kv_width)
    served, new_pool = serve_owner(dec_query, dec_keyval, dec_lengths, dec_pool)
    back = tree_gather(served)
    got_ids = got[:, q_width + 2 * kv_width:used].astype(jnp.int32)
    requests = got_ids[:, 0] * dec_count + got_ids[:, 1]
    wanted = tok_place * dec_count + jnp.arange(dec_count, dtype=jnp.int32)
    where = jnp.argmax(requests[None, :] == wanted[:, None], axis=1)
    dec_attn = jnp.take(back, where, axis=0)
    all_query, all_keyval = project(pre_tokens, w_query, kv_weight, b_query, kv_bias)
    half_id = tok_place % 2
    offset = pre_offsets[tok_place // 2]
    local_pos = jnp.arange(pre_count, dtype=jnp.int32)
    positions = offset + half_id * pre_count + local_pos
    q_heads = q_width // HD
    kv_heads = kv_width // HD
    turned = rotate(all_query.reshape(pre_count, q_heads, HD), positions)
    turned = turned.astype(jnp.bfloat16).reshape(pre_count, q_width)
    pre_kv = all_keyval.reshape(pre_count, 2, kv_width)
    new_keys = rotate(pre_kv[:, 0].reshape(pre_count, kv_heads, HD), positions)
    new_keys = new_keys.astype(jnp.bfloat16).reshape(pre_count, kv_width)
    appended = jnp.stack([new_keys, pre_kv[:, 1].astype(jnp.bfloat16)], axis=0)
    shard = pre_cache.shape[1]
    other_cache, other_new = swapped((pre_cache, appended), "tok", 0)
    is_lower = half_id == 0
    history = jnp.where(
        is_lower,
        jnp.concatenate([pre_cache, other_cache], axis=1),
        jnp.concatenate([other_cache, pre_cache], axis=1),
    )
    block_rows = jnp.where(
        is_lower,
        jnp.concatenate([appended, other_new], axis=1),
        jnp.concatenate([other_new, appended], axis=1),
    )
    key_rows = jnp.concatenate([history, block_rows], axis=1)
    key_slots = jnp.arange(key_rows.shape[1], dtype=jnp.int32)
    key_pos = jnp.where(key_slots < 2 * shard, key_slots, offset + key_slots - 2 * shard)
    usable = (key_slots < offset) | (key_slots >= 2 * shard)
    allowed = usable[None, :] & (key_pos[None, :] <= positions[:, None])
    scores = head_scores(turned, key_rows[0], allowed)
    totals, mixed = head_mix(scores, jnp.max(scores, axis=-1), key_rows[1])
    pre_attn = (mixed / totals[..., None]).astype(jnp.bfloat16).reshape(pre_count, q_width)
    return (dec_attn, pre_attn, new_pool, appended)


def solution(mesh):
    in_specs = (
        P("tok", "kv"),
        P("tok", "kv"),
        P(None, "kv"),
        P(None, None, "kv"),
        P("kv"),
        P(None, "kv"),
        P(None, "tok", "kv"),
        P("tok"),
        P("tok"),
        P(None, "tok", "kv"),
        P(),
    )
    out_specs = (P("tok", "kv"), P("tok", "kv"), P(None, "tok", "kv"), P(None, "tok", "kv"))
    return jax.shard_map(body, mesh=mesh, in_specs=in_specs, out_specs=out_specs, check_vma=False)
```

```python
import jax
import jax.numpy as jnp
from jax import lax
from jax.sharding import PartitionSpec as P

HD = 128


THETA = 1000000.0


def swapped(value, axis, distance):
    return lax.ppermute(value, axis, [(i, i ^ 1 << distance) for i in range(lax.axis_size(axis))])


def rotate(values, positions):
    halfway = values.shape[-1] // 2
    spread = jnp.arange(halfway, dtype=jnp.float32) * (2.0 / values.shape[-1])
    rates = jnp.power(jnp.float32(THETA), -spread)
    angles = positions.astype(jnp.float32)[:, None] * rates[None, :]
    cosine = jnp.cos(angles)[:, None, :]
    sine = jnp.sin(angles)[:, None, :]
    former = values[..., :halfway]
    latter = values[..., halfway:]
    return jnp.concatenate(
        [former * cosine - latter * sine, latter * cosine + former * sine], axis=-1
    )


def head_scores(queries, key_rows, allowed):
    amount = queries.shape[0]
    q_heads = queries.shape[1] // HD
    shaped = queries.reshape(amount, q_heads, HD)
    product = jnp.einsum("ngd,md->ngm", shaped, key_rows, preferred_element_type=jnp.float32)
    scores = product * HD ** (-0.5)
    return jnp.where(allowed[:, None, :], scores, -jnp.inf)


def head_mix(scores, peaks, value_rows):
    powers = jnp.exp(scores - peaks[..., None])
    totals = jnp.sum(powers, axis=-1)
    weights = powers.astype(jnp.bfloat16)
    product = jnp.einsum("ngm,md->ngd", weights, value_rows, preferred_element_type=jnp.float32)
    return (totals, product)


def serve_owner(queries, keyval, lengths, cache_pool):
    amount = queries.shape[0]
    q_heads = queries.shape[1] // HD
    kv_heads = cache_pool.shape[2] // HD
    finish = jnp.cumsum(lengths + 1)
    starts = finish - lengths - 1
    turned = rotate(queries.astype(jnp.float32).reshape(amount, q_heads, HD), lengths)
    turned = turned.astype(jnp.bfloat16).reshape(amount, q_heads * HD)
    new_keys = rotate(keyval[:, 0].astype(jnp.float32).reshape(amount, kv_heads, HD), lengths)
    new_keys = new_keys.astype(jnp.bfloat16).reshape(amount, kv_heads * HD)
    appended = jnp.stack([new_keys, keyval[:, 1]], axis=0)
    cache_pool = cache_pool.at[:, starts + lengths].set(appended)
    spots = jnp.arange(cache_pool.shape[1], dtype=jnp.int32)
    allowed = (spots[None, :] >= starts[:, None]) & (spots[None, :] <= (starts + lengths)[:, None])
    scores = head_scores(turned, cache_pool[0], allowed)
    totals, mixed = head_mix(scores, jnp.max(scores, axis=-1), cache_pool[1])
    result = (mixed / totals[..., None]).astype(jnp.bfloat16).reshape(amount, q_heads * HD)
    return (result, cache_pool)


def tree_gather(value):
    buffer = value
    for stride, count in ((1, 2), (2, 4), (8, 4)):
      parts = [buffer]
      for shift in range(1, count):
          pairs = []
          for i in range(32):
              digit = (i // stride) % count
              target = i + (((digit + shift) % count) - digit) * stride
              pairs.append((i, target))
          parts.append(lax.ppermute(buffer, "tok", pairs))
      buffer = jnp.concatenate(parts, axis=0)
    return buffer


def tree_row(place, source, rows):
    core = (place % 2) ^ (source % 2)
    y = ((place // 2) % 4 - (source // 2) % 4) % 4
    z = (place // 8 - source // 8) % 4
    return ((z * 4 + y) * 2 + core) * rows


def project(rows, w_query, kv_weight, b_query, kv_bias):
    cols = lax.all_gather(rows, "kv", axis=1, tiled=True)
    query = jnp.dot(cols, w_query, preferred_element_type=jnp.float32) + b_query
    keyval = jnp.dot(cols, kv_weight, preferred_element_type=jnp.float32) + kv_bias
    return query, keyval


def body_inner(dec_tokens, pre_tokens, w_query, w_keyval, b_query, b_keyval, dec_pool, owner_slots, dec_lengths):
    dec_count = dec_tokens.shape[0]
    q_width = w_query.shape[1]
    kv_width = w_keyval.shape[2]
    kv_weight = w_keyval.reshape(w_keyval.shape[0], 2 * kv_width)
    kv_bias = b_keyval.reshape(2 * kv_width)
    dec_q, dec_kv = project(dec_tokens, w_query, kv_weight, b_query, kv_bias)
    tok_place = lax.axis_index("tok")
    ids = jnp.stack([owner_slots // dec_count, owner_slots % dec_count], axis=1).astype(jnp.bfloat16)
    used = q_width + 2 * kv_width + 2
    pad = jnp.zeros((dec_count, -(-used // 128) * 128 - used), jnp.bfloat16)
    sent = jnp.concatenate([dec_q.astype(jnp.bfloat16), dec_kv.astype(jnp.bfloat16), ids, pad], axis=1)
    got = tree_gather(sent)
    rows = tree_row(tok_place, owner_slots // dec_count, dec_count) + owner_slots % dec_count
    chosen = jnp.take(got, rows, axis=0)
    dec_query = chosen[:, :q_width]
    dec_keyval = chosen[:, q_width:q_width + 2 * kv_width].reshape(dec_count, 2, kv_width)
    served, new_pool = serve_owner(dec_query, dec_keyval, dec_lengths, dec_pool)
    back = tree_gather(served)
    got_ids = got[:, q_width + 2 * kv_width:used].astype(jnp.int32)
    requests = got_ids[:, 0] * dec_count + got_ids[:, 1]
    wanted = tok_place * dec_count + jnp.arange(dec_count, dtype=jnp.int32)
    where = jnp.argmax(requests[None, :] == wanted[:, None], axis=1)
    dec_attn = jnp.take(back, where, axis=0)
    all_query, all_keyval = project(pre_tokens, w_query, kv_weight, b_query, kv_bias)
    return dec_attn, new_pool, all_query, all_keyval


def prefill(all_query, all_keyval, pre_tokens, w_query, w_keyval, pre_cache, pre_offsets):
    pre_count = pre_tokens.shape[0]
    q_width = w_query.shape[1]
    kv_width = w_keyval.shape[2]
    tok_place = lax.axis_index("tok")
    half_id = tok_place % 2
    offset = pre_offsets[tok_place // 2]
    local_pos = jnp.arange(pre_count, dtype=jnp.int32)
    positions = offset + half_id * pre_count + local_pos
    q_heads = q_width // HD
    kv_heads = kv_width // HD
    turned = rotate(all_query.reshape(pre_count, q_heads, HD), positions)
    turned = turned.astype(jnp.bfloat16).reshape(pre_count, q_width)
    pre_kv = all_keyval.reshape(pre_count, 2, kv_width)
    new_keys = rotate(pre_kv[:, 0].reshape(pre_count, kv_heads, HD), positions)
    new_keys = new_keys.astype(jnp.bfloat16).reshape(pre_count, kv_width)
    appended = jnp.stack([new_keys, pre_kv[:, 1].astype(jnp.bfloat16)], axis=0)
    shard = pre_cache.shape[1]
    other_cache, other_new = swapped((pre_cache, appended), "tok", 0)
    is_lower = half_id == 0
    history = jnp.where(
        is_lower,
        jnp.concatenate([pre_cache, other_cache], axis=1),
        jnp.concatenate([other_cache, pre_cache], axis=1),
    )
    block_rows = jnp.where(
        is_lower,
        jnp.concatenate([appended, other_new], axis=1),
        jnp.concatenate([other_new, appended], axis=1),
    )
    key_rows = jnp.concatenate([history, block_rows], axis=1)
    key_slots = jnp.arange(key_rows.shape[1], dtype=jnp.int32)
    key_pos = jnp.where(key_slots < 2 * shard, key_slots, offset + key_slots - 2 * shard)
    usable = (key_slots < offset) | (key_slots >= 2 * shard)
    allowed = usable[None, :] & (key_pos[None, :] <= positions[:, None])
    scores = head_scores(turned, key_rows[0], allowed)
    totals, mixed = head_mix(scores, jnp.max(scores, axis=-1), key_rows[1])
    pre_attn = (mixed / totals[..., None]).astype(jnp.bfloat16).reshape(pre_count, q_width)
    return pre_attn, appended


def body(dec_tokens, pre_tokens, w_query, w_keyval, b_query, b_keyval, dec_pool, owner_slots, dec_lengths, pre_cache, pre_offsets):
    dec_attn, new_pool, all_query, all_keyval = body_inner(
        dec_tokens, pre_tokens, w_query, w_keyval, b_query, b_keyval, dec_pool, owner_slots, dec_lengths
    )
    pre_attn, appended = prefill(all_query, all_keyval, pre_tokens, w_query, w_keyval, pre_cache, pre_offsets)
    return (dec_attn, pre_attn, new_pool, appended)


def solution(mesh):
    in_specs = (
        P("tok", "kv"),
        P("tok", "kv"),
        P(None, "kv"),
        P(None, None, "kv"),
        P("kv"),
        P(None, "kv"),
        P(None, "tok", "kv"),
        P("tok"),
        P("tok"),
        P(None, "tok", "kv"),
        P(),
    )
    out_specs = (P("tok", "kv"), P("tok", "kv"), P(None, "tok", "kv"), P(None, "tok", "kv"))
    return jax.shard_map(body, mesh=mesh, in_specs=in_specs, out_specs=out_specs, check_vma=False)
```

```python
import jax
import jax.numpy as jnp
from jax import lax
from jax.sharding import PartitionSpec as P

HD = 128


THETA = 1000000.0


def swapped(value, axis, distance):
    return lax.ppermute(value, axis, [(i, i ^ 1 << distance) for i in range(lax.axis_size(axis))])


def rotate(values, positions):
    halfway = values.shape[-1] // 2
    spread = jnp.arange(halfway, dtype=jnp.float32) * (2.0 / values.shape[-1])
    rates = jnp.power(jnp.float32(THETA), -spread)
    angles = positions.astype(jnp.float32)[:, None] * rates[None, :]
    cosine = jnp.cos(angles)[:, None, :]
    sine = jnp.sin(angles)[:, None, :]
    former = values[..., :halfway]
    latter = values[..., halfway:]
    return jnp.concatenate(
        [former * cosine - latter * sine, latter * cosine + former * sine], axis=-1
    )


def head_scores(queries, key_rows, allowed):
    amount = queries.shape[0]
    q_heads = queries.shape[1] // HD
    shaped = queries.reshape(amount, q_heads, HD)
    product = jnp.einsum("ngd,md->ngm", shaped, key_rows, preferred_element_type=jnp.float32)
    scores = product * HD ** (-0.5)
    return jnp.where(allowed[:, None, :], scores, -jnp.inf)


def head_mix(scores, peaks, value_rows):
    powers = jnp.exp(scores - peaks[..., None])
    totals = jnp.sum(powers, axis=-1)
    weights = powers.astype(jnp.bfloat16)
    product = jnp.einsum("ngm,md->ngd", weights, value_rows, preferred_element_type=jnp.float32)
    return (totals, product)


def serve_owner(queries, keyval, lengths, cache_pool):
    amount = queries.shape[0]
    q_heads = queries.shape[1] // HD
    kv_heads = cache_pool.shape[2] // HD
    finish = jnp.cumsum(lengths + 1)
    starts = finish - lengths - 1
    turned = rotate(queries.astype(jnp.float32).reshape(amount, q_heads, HD), lengths)
    turned = turned.astype(jnp.bfloat16).reshape(amount, q_heads * HD)
    new_keys = rotate(keyval[:, 0].astype(jnp.float32).reshape(amount, kv_heads, HD), lengths)
    new_keys = new_keys.astype(jnp.bfloat16).reshape(amount, kv_heads * HD)
    appended = jnp.stack([new_keys, keyval[:, 1]], axis=0)
    cache_pool = cache_pool.at[:, starts + lengths].set(appended)
    spots = jnp.arange(cache_pool.shape[1], dtype=jnp.int32)
    allowed = (spots[None, :] >= starts[:, None]) & (spots[None, :] <= (starts + lengths)[:, None])
    scores = head_scores(turned, cache_pool[0], allowed)
    totals, mixed = head_mix(scores, jnp.max(scores, axis=-1), cache_pool[1])
    result = (mixed / totals[..., None]).astype(jnp.bfloat16).reshape(amount, q_heads * HD)
    return (result, cache_pool)


def tree_gather(value):
    buffer = value
    for stride, count in ((1, 2), (2, 4), (8, 4)):
      parts = [buffer]
      for shift in range(1, count):
          pairs = []
          for i in range(32):
              digit = (i // stride) % count
              target = i + (((digit + shift) % count) - digit) * stride
              pairs.append((i, target))
          parts.append(lax.ppermute(buffer, "tok", pairs))
      buffer = jnp.concatenate(parts, axis=0)
    return buffer


def tree_row(place, source, rows):
    core = (place % 2) ^ (source % 2)
    y = ((place // 2) % 4 - (source // 2) % 4) % 4
    z = (place // 8 - source // 8) % 4
    return ((z * 4 + y) * 2 + core) * rows


def ring_columns(rows):
    count = lax.axis_size("kv")
    place = lax.axis_index("kv")
    parts = [rows] + [lax.ppermute(rows, "kv", [(i, (i + s) % count) for i in range(count)]) for s in range(1, count)]
    ordered = jnp.take(jnp.stack(parts), (place - jnp.arange(count)) % count, axis=0)
    return jnp.transpose(ordered, (1, 0, 2)).reshape(rows.shape[0], count * rows.shape[1])


def project(rows, w_query, kv_weight, b_query, kv_bias, ring=False):
    cols = ring_columns(rows) if ring else lax.all_gather(rows, "kv", axis=1, tiled=True)
    query = jnp.dot(cols, w_query, preferred_element_type=jnp.float32) + b_query
    keyval = jnp.dot(cols, kv_weight, preferred_element_type=jnp.float32) + kv_bias
    return query, keyval


def body_inner(dec_tokens, pre_tokens, w_query, w_keyval, b_query, b_keyval, dec_pool, owner_slots, dec_lengths):
    dec_count = dec_tokens.shape[0]
    q_width = w_query.shape[1]
    kv_width = w_keyval.shape[2]
    kv_weight = w_keyval.reshape(w_keyval.shape[0], 2 * kv_width)
    kv_bias = b_keyval.reshape(2 * kv_width)
    dec_q, dec_kv = project(dec_tokens, w_query, kv_weight, b_query, kv_bias, ring=True)
    tok_place = lax.axis_index("tok")
    ids = jnp.stack([owner_slots // dec_count, owner_slots % dec_count], axis=1).astype(jnp.bfloat16)
    used = q_width + 2 * kv_width + 2
    pad = jnp.zeros((dec_count, -(-used // 128) * 128 - used), jnp.bfloat16)
    sent = jnp.concatenate([dec_q.astype(jnp.bfloat16), dec_kv.astype(jnp.bfloat16), ids, pad], axis=1)
    got = tree_gather(sent)
    rows = tree_row(tok_place, owner_slots // dec_count, dec_count) + owner_slots % dec_count
    chosen = jnp.take(got, rows, axis=0)
    dec_query = chosen[:, :q_width]
    dec_keyval = chosen[:, q_width:q_width + 2 * kv_width].reshape(dec_count, 2, kv_width)
    served, new_pool = serve_owner(dec_query, dec_keyval, dec_lengths, dec_pool)
    back = tree_gather(served)
    got_ids = got[:, q_width + 2 * kv_width:used].astype(jnp.int32)
    requests = got_ids[:, 0] * dec_count + got_ids[:, 1]
    wanted = tok_place * dec_count + jnp.arange(dec_count, dtype=jnp.int32)
    where = jnp.argmax(requests[None, :] == wanted[:, None], axis=1)
    dec_attn = jnp.take(back, where, axis=0)
    all_query, all_keyval = project(pre_tokens, w_query, kv_weight, b_query, kv_bias)
    return dec_attn, new_pool, all_query, all_keyval


def prefill(all_query, all_keyval, pre_tokens, w_query, w_keyval, pre_cache, pre_offsets):
    pre_count = pre_tokens.shape[0]
    q_width = w_query.shape[1]
    kv_width = w_keyval.shape[2]
    tok_place = lax.axis_index("tok")
    half_id = tok_place % 2
    offset = pre_offsets[tok_place // 2]
    local_pos = jnp.arange(pre_count, dtype=jnp.int32)
    positions = offset + half_id * pre_count + local_pos
    q_heads = q_width // HD
    kv_heads = kv_width // HD
    turned = rotate(all_query.reshape(pre_count, q_heads, HD), positions)
    turned = turned.astype(jnp.bfloat16).reshape(pre_count, q_width)
    pre_kv = all_keyval.reshape(pre_count, 2, kv_width)
    new_keys = rotate(pre_kv[:, 0].reshape(pre_count, kv_heads, HD), positions)
    new_keys = new_keys.astype(jnp.bfloat16).reshape(pre_count, kv_width)
    appended = jnp.stack([new_keys, pre_kv[:, 1].astype(jnp.bfloat16)], axis=0)
    shard = pre_cache.shape[1]
    other_cache, other_new = swapped((pre_cache, appended), "tok", 0)
    is_lower = half_id == 0
    history = jnp.where(
        is_lower,
        jnp.concatenate([pre_cache, other_cache], axis=1),
        jnp.concatenate([other_cache, pre_cache], axis=1),
    )
    block_rows = jnp.where(
        is_lower,
        jnp.concatenate([appended, other_new], axis=1),
        jnp.concatenate([other_new, appended], axis=1),
    )
    key_rows = jnp.concatenate([history, block_rows], axis=1)
    key_slots = jnp.arange(key_rows.shape[1], dtype=jnp.int32)
    key_pos = jnp.where(key_slots < 2 * shard, key_slots, offset + key_slots - 2 * shard)
    usable = (key_slots < offset) | (key_slots >= 2 * shard)
    allowed = usable[None, :] & (key_pos[None, :] <= positions[:, None])
    scores = head_scores(turned, key_rows[0], allowed)
    totals, mixed = head_mix(scores, jnp.max(scores, axis=-1), key_rows[1])
    pre_attn = (mixed / totals[..., None]).astype(jnp.bfloat16).reshape(pre_count, q_width)
    return pre_attn, appended


def body(dec_tokens, pre_tokens, w_query, w_keyval, b_query, b_keyval, dec_pool, owner_slots, dec_lengths, pre_cache, pre_offsets):
    dec_attn, new_pool, all_query, all_keyval = body_inner(
        dec_tokens, pre_tokens, w_query, w_keyval, b_query, b_keyval, dec_pool, owner_slots, dec_lengths
    )
    pre_attn, appended = prefill(all_query, all_keyval, pre_tokens, w_query, w_keyval, pre_cache, pre_offsets)
    return (dec_attn, pre_attn, new_pool, appended)


def solution(mesh):
    in_specs = (
        P("tok", "kv"),
        P("tok", "kv"),
        P(None, "kv"),
        P(None, None, "kv"),
        P("kv"),
        P(None, "kv"),
        P(None, "tok", "kv"),
        P("tok"),
        P("tok"),
        P(None, "tok", "kv"),
        P(),
    )
    out_specs = (P("tok", "kv"), P("tok", "kv"), P(None, "tok", "kv"), P(None, "tok", "kv"))
    return jax.shard_map(body, mesh=mesh, in_specs=in_specs, out_specs=out_specs, check_vma=False)
```

```python
import jax
import jax.numpy as jnp
from jax import lax
from jax.sharding import PartitionSpec as P
from jax.experimental import pallas as pl

HD = 128


THETA = 1000000.0


def swapped(value, axis, distance):
    return lax.ppermute(value, axis, [(i, i ^ 1 << distance) for i in range(lax.axis_size(axis))])


def rotate(values, positions):
    halfway = values.shape[-1] // 2
    spread = jnp.arange(halfway, dtype=jnp.float32) * (2.0 / values.shape[-1])
    rates = jnp.power(jnp.float32(THETA), -spread)
    angles = positions.astype(jnp.float32)[:, None] * rates[None, :]
    cosine = jnp.cos(angles)[:, None, :]
    sine = jnp.sin(angles)[:, None, :]
    former = values[..., :halfway]
    latter = values[..., halfway:]
    return jnp.concatenate(
        [former * cosine - latter * sine, latter * cosine + former * sine], axis=-1
    )


def attend_kernel(q_ref, k_ref, v_ref, qpos_ref, kpos_ref, o_ref):
    scores = lax.dot_general(
        q_ref[...], k_ref[...], (((1,), (1,)), ((), ())), preferred_element_type=jnp.float32
    ) * HD ** (-0.5)
    allowed = kpos_ref[...] <= qpos_ref[...]
    scores = jnp.where(allowed, scores, -jnp.inf)
    top = jnp.max(scores, axis=1, keepdims=True)
    powers = jnp.exp(scores - top)
    total = jnp.sum(powers, axis=1, keepdims=True)
    mixed = jnp.dot(powers.astype(jnp.bfloat16), v_ref[...], preferred_element_type=jnp.float32)
    o_ref[...] = (mixed / total).astype(o_ref.dtype)


def attend(queries, keys, values, query_pos, key_pos):
    amount, width = queries.shape
    length = keys.shape[0]
    return pl.pallas_call(
        attend_kernel,
        grid=(width // HD,),
        in_specs=[
            pl.BlockSpec((amount, HD), lambda h: (0, h)),
            pl.BlockSpec((length, HD), lambda h: (0, 0)),
            pl.BlockSpec((length, HD), lambda h: (0, 0)),
            pl.BlockSpec((amount, 1), lambda h: (0, 0)),
            pl.BlockSpec((1, length), lambda h: (0, 0)),
        ],
        out_specs=pl.BlockSpec((amount, HD), lambda h: (0, h)),
        out_shape=jax.ShapeDtypeStruct((amount, width), jnp.bfloat16),
    )(queries, keys, values, query_pos.reshape(amount, 1), key_pos.reshape(1, length))


def head_scores(queries, key_rows, allowed):
    amount = queries.shape[0]
    q_heads = queries.shape[1] // HD
    shaped = queries.reshape(amount, q_heads, HD)
    product = jnp.einsum("ngd,md->ngm", shaped, key_rows, preferred_element_type=jnp.float32)
    scores = product * HD ** (-0.5)
    return jnp.where(allowed[:, None, :], scores, -jnp.inf)


def head_mix(scores, peaks, value_rows):
    powers = jnp.exp(scores - peaks[..., None])
    totals = jnp.sum(powers, axis=-1)
    weights = powers.astype(jnp.bfloat16)
    product = jnp.einsum("ngm,md->ngd", weights, value_rows, preferred_element_type=jnp.float32)
    return (totals, product)


def serve_owner(queries, keyval, lengths, cache_pool):
    amount = queries.shape[0]
    q_heads = queries.shape[1] // HD
    kv_heads = cache_pool.shape[2] // HD
    finish = jnp.cumsum(lengths + 1)
    starts = finish - lengths - 1
    turned = rotate(queries.astype(jnp.float32).reshape(amount, q_heads, HD), lengths)
    turned = turned.astype(jnp.bfloat16).reshape(amount, q_heads * HD)
    new_keys = rotate(keyval[:, 0].astype(jnp.float32).reshape(amount, kv_heads, HD), lengths)
    new_keys = new_keys.astype(jnp.bfloat16).reshape(amount, kv_heads * HD)
    appended = jnp.stack([new_keys, keyval[:, 1]], axis=0)
    cache_pool = cache_pool.at[:, starts + lengths].set(appended)
    spots = jnp.arange(cache_pool.shape[1], dtype=jnp.int32)
    allowed = (spots[None, :] >= starts[:, None]) & (spots[None, :] <= (starts + lengths)[:, None])
    scores = head_scores(turned, cache_pool[0], allowed)
    totals, mixed = head_mix(scores, jnp.max(scores, axis=-1), cache_pool[1])
    result = (mixed / totals[..., None]).astype(jnp.bfloat16).reshape(amount, q_heads * HD)
    return (result, cache_pool)


def tree_gather(value):
    buffer = value
    for stride, count in ((1, 2), (2, 4), (8, 4)):
      parts = [buffer]
      for shift in range(1, count):
          pairs = []
          for i in range(32):
              digit = (i // stride) % count
              target = i + (((digit + shift) % count) - digit) * stride
              pairs.append((i, target))
          parts.append(lax.ppermute(buffer, "tok", pairs))
      buffer = jnp.concatenate(parts, axis=0)
    return buffer


def tree_row(place, source, rows):
    core = (place % 2) ^ (source % 2)
    y = ((place // 2) % 4 - (source // 2) % 4) % 4
    z = (place // 8 - source // 8) % 4
    return ((z * 4 + y) * 2 + core) * rows


def project(rows, w_query, kv_weight, b_query, kv_bias):
    cols = lax.all_gather(rows, "kv", axis=1, tiled=True)
    query = jnp.dot(cols, w_query, preferred_element_type=jnp.float32) + b_query
    keyval = jnp.dot(cols, kv_weight, preferred_element_type=jnp.float32) + kv_bias
    return query, keyval


def body_inner(dec_tokens, pre_tokens, w_query, w_keyval, b_query, b_keyval, dec_pool, owner_slots, dec_lengths):
    dec_count = dec_tokens.shape[0]
    q_width = w_query.shape[1]
    kv_width = w_keyval.shape[2]
    kv_weight = w_keyval.reshape(w_keyval.shape[0], 2 * kv_width)
    kv_bias = b_keyval.reshape(2 * kv_width)
    dec_q, dec_kv = project(dec_tokens, w_query, kv_weight, b_query, kv_bias)
    tok_place = lax.axis_index("tok")
    ids = jnp.stack([owner_slots // dec_count, owner_slots % dec_count], axis=1).astype(jnp.bfloat16)
    used = q_width + 2 * kv_width + 2
    pad = jnp.zeros((dec_count, -(-used // 128) * 128 - used), jnp.bfloat16)
    sent = jnp.concatenate([dec_q.astype(jnp.bfloat16), dec_kv.astype(jnp.bfloat16), ids, pad], axis=1)
    got = tree_gather(sent)
    rows = tree_row(tok_place, owner_slots // dec_count, dec_count) + owner_slots % dec_count
    chosen = jnp.take(got, rows, axis=0)
    dec_query = chosen[:, :q_width]
    dec_keyval = chosen[:, q_width:q_width + 2 * kv_width].reshape(dec_count, 2, kv_width)
    served, new_pool = serve_owner(dec_query, dec_keyval, dec_lengths, dec_pool)
    back = tree_gather(served)
    got_ids = got[:, q_width + 2 * kv_width:used].astype(jnp.int32)
    requests = got_ids[:, 0] * dec_count + got_ids[:, 1]
    wanted = tok_place * dec_count + jnp.arange(dec_count, dtype=jnp.int32)
    where = jnp.argmax(requests[None, :] == wanted[:, None], axis=1)
    dec_attn = jnp.take(back, where, axis=0)
    all_query, all_keyval = project(pre_tokens, w_query, kv_weight, b_query, kv_bias)
    return dec_attn, new_pool, all_query, all_keyval


def prefill(all_query, all_keyval, pre_tokens, w_query, w_keyval, pre_cache, pre_offsets):
    pre_count = pre_tokens.shape[0]
    q_width = w_query.shape[1]
    kv_width = w_keyval.shape[2]
    tok_place = lax.axis_index("tok")
    half_id = tok_place % 2
    offset = pre_offsets[tok_place // 2]
    local_pos = jnp.arange(pre_count, dtype=jnp.int32)
    positions = offset + half_id * pre_count + local_pos
    q_heads = q_width // HD
    kv_heads = kv_width // HD
    turned = rotate(all_query.reshape(pre_count, q_heads, HD), positions)
    turned = turned.astype(jnp.bfloat16).reshape(pre_count, q_width)
    pre_kv = all_keyval.reshape(pre_count, 2, kv_width)
    new_keys = rotate(pre_kv[:, 0].reshape(pre_count, kv_heads, HD), positions)
    new_keys = new_keys.astype(jnp.bfloat16).reshape(pre_count, kv_width)
    appended = jnp.stack([new_keys, pre_kv[:, 1].astype(jnp.bfloat16)], axis=0)
    shard = pre_cache.shape[1]
    other_cache, other_new = swapped((pre_cache, appended), "tok", 0)
    is_lower = half_id == 0
    history = jnp.where(
        is_lower,
        jnp.concatenate([pre_cache, other_cache], axis=1),
        jnp.concatenate([other_cache, pre_cache], axis=1),
    )
    block_rows = jnp.where(
        is_lower,
        jnp.concatenate([appended, other_new], axis=1),
        jnp.concatenate([other_new, appended], axis=1),
    )
    key_rows = jnp.concatenate([history, block_rows], axis=1)
    key_slots = jnp.arange(key_rows.shape[1], dtype=jnp.int32)
    key_pos = jnp.where(key_slots < 2 * shard, key_slots, offset + key_slots - 2 * shard)
    usable = (key_slots < offset) | (key_slots >= 2 * shard)
    key_pos = jnp.where(usable, key_pos, jnp.int32(1 << 30))
    pre_attn = attend(turned, key_rows[0], key_rows[1], positions, key_pos)
    return pre_attn, appended


def body(dec_tokens, pre_tokens, w_query, w_keyval, b_query, b_keyval, dec_pool, owner_slots, dec_lengths, pre_cache, pre_offsets):
    dec_attn, new_pool, all_query, all_keyval = body_inner(
        dec_tokens, pre_tokens, w_query, w_keyval, b_query, b_keyval, dec_pool, owner_slots, dec_lengths
    )
    pre_attn, appended = prefill(all_query, all_keyval, pre_tokens, w_query, w_keyval, pre_cache, pre_offsets)
    return (dec_attn, pre_attn, new_pool, appended)


def solution(mesh):
    in_specs = (
        P("tok", "kv"),
        P("tok", "kv"),
        P(None, "kv"),
        P(None, None, "kv"),
        P("kv"),
        P(None, "kv"),
        P(None, "tok", "kv"),
        P("tok"),
        P("tok"),
        P(None, "tok", "kv"),
        P(),
    )
    out_specs = (P("tok", "kv"), P("tok", "kv"), P(None, "tok", "kv"), P(None, "tok", "kv"))
    return jax.shard_map(body, mesh=mesh, in_specs=in_specs, out_specs=out_specs, check_vma=False)
```

```python
import jax
import jax.numpy as jnp
from jax import lax
from jax.sharding import PartitionSpec as P
from jax.experimental import pallas as pl

HD = 128


THETA = 1000000.0


def swapped(value, axis, distance):
    return lax.ppermute(value, axis, [(i, i ^ 1 << distance) for i in range(lax.axis_size(axis))])


def rotate(values, positions):
    halfway = values.shape[-1] // 2
    spread = jnp.arange(halfway, dtype=jnp.float32) * (2.0 / values.shape[-1])
    rates = jnp.power(jnp.float32(THETA), -spread)
    angles = positions.astype(jnp.float32)[:, None] * rates[None, :]
    cosine = jnp.cos(angles)[:, None, :]
    sine = jnp.sin(angles)[:, None, :]
    former = values[..., :halfway]
    latter = values[..., halfway:]
    return jnp.concatenate(
        [former * cosine - latter * sine, latter * cosine + former * sine], axis=-1
    )


def attend_kernel(q_ref, k_ref, v_ref, qpos_ref, kpos_ref, o_ref):
    scores = lax.dot_general(
        q_ref[...], k_ref[...], (((1,), (1,)), ((), ())), preferred_element_type=jnp.float32
    ) * HD ** (-0.5)
    allowed = kpos_ref[...] <= qpos_ref[...]
    scores = jnp.where(allowed, scores, -jnp.inf)
    top = jnp.max(scores, axis=1, keepdims=True)
    powers = jnp.exp(scores - top)
    total = jnp.sum(powers, axis=1, keepdims=True)
    mixed = jnp.dot(powers.astype(jnp.bfloat16), v_ref[...], preferred_element_type=jnp.float32)
    o_ref[...] = (mixed / total).astype(o_ref.dtype)


def attend(queries, keys, values, query_pos, key_pos):
    amount, width = queries.shape
    length = keys.shape[0]
    return pl.pallas_call(
        attend_kernel,
        grid=(width // HD,),
        in_specs=[
            pl.BlockSpec((amount, HD), lambda h: (0, h)),
            pl.BlockSpec((length, HD), lambda h: (0, 0)),
            pl.BlockSpec((length, HD), lambda h: (0, 0)),
            pl.BlockSpec((amount, 1), lambda h: (0, 0)),
            pl.BlockSpec((1, length), lambda h: (0, 0)),
        ],
        out_specs=pl.BlockSpec((amount, HD), lambda h: (0, h)),
        out_shape=jax.ShapeDtypeStruct((amount, width), jnp.bfloat16),
    )(queries, keys, values, query_pos.reshape(amount, 1), key_pos.reshape(1, length))


def head_scores(queries, key_rows, allowed):
    amount = queries.shape[0]
    q_heads = queries.shape[1] // HD
    shaped = queries.reshape(amount, q_heads, HD)
    product = jnp.einsum("ngd,md->ngm", shaped, key_rows, preferred_element_type=jnp.float32)
    scores = product * HD ** (-0.5)
    return jnp.where(allowed[:, None, :], scores, -jnp.inf)


def head_mix(scores, peaks, value_rows):
    powers = jnp.exp(scores - peaks[..., None])
    totals = jnp.sum(powers, axis=-1)
    weights = powers.astype(jnp.bfloat16)
    product = jnp.einsum("ngm,md->ngd", weights, value_rows, preferred_element_type=jnp.float32)
    return (totals, product)


def serve_owner(queries, keyval, lengths, cache_pool):
    amount = queries.shape[0]
    q_heads = queries.shape[1] // HD
    kv_heads = cache_pool.shape[2] // HD
    finish = jnp.cumsum(lengths + 1)
    starts = finish - lengths - 1
    turned = rotate(queries.astype(jnp.float32).reshape(amount, q_heads, HD), lengths)
    turned = turned.astype(jnp.bfloat16).reshape(amount, q_heads * HD)
    new_keys = rotate(keyval[:, 0].astype(jnp.float32).reshape(amount, kv_heads, HD), lengths)
    new_keys = new_keys.astype(jnp.bfloat16).reshape(amount, kv_heads * HD)
    new_values = keyval[:, 1]
    appended = jnp.stack([new_keys, new_values], axis=0)
    new_pool = cache_pool.at[:, starts + lengths].set(appended)
    spots = jnp.arange(cache_pool.shape[1], dtype=jnp.int32)
    allowed = (spots[None, :] >= starts[:, None]) & (spots[None, :] < (starts + lengths)[:, None])
    scores = head_scores(turned, cache_pool[0], allowed)
    fresh = jnp.einsum(
        "ngd,nd->ng", turned.reshape(amount, q_heads, HD), new_keys, preferred_element_type=jnp.float32
    ) * HD ** (-0.5)
    top = jnp.maximum(jnp.max(scores, axis=-1), fresh)
    totals, mixed = head_mix(scores, top, cache_pool[1])
    fresh_power = jnp.exp(fresh - top)
    totals = totals + fresh_power
    fresh_weight = fresh_power.astype(jnp.bfloat16).astype(jnp.float32)
    mixed = mixed + fresh_weight[..., None] * new_values.astype(jnp.float32)[:, None, :]
    result = (mixed / totals[..., None]).astype(jnp.bfloat16).reshape(amount, q_heads * HD)
    return (result, new_pool)


def tree_gather(value):
    buffer = value
    for stride, count in ((1, 2), (2, 4), (8, 4)):
      parts = [buffer]
      for shift in range(1, count):
          pairs = []
          for i in range(32):
              digit = (i // stride) % count
              target = i + (((digit + shift) % count) - digit) * stride
              pairs.append((i, target))
          parts.append(lax.ppermute(buffer, "tok", pairs))
      buffer = jnp.concatenate(parts, axis=0)
    return buffer


def tree_row(place, source, rows):
    core = (place % 2) ^ (source % 2)
    y = ((place // 2) % 4 - (source // 2) % 4) % 4
    z = (place // 8 - source // 8) % 4
    return ((z * 4 + y) * 2 + core) * rows


def project(rows, w_query, kv_weight, b_query, kv_bias):
    cols = lax.all_gather(rows, "kv", axis=1, tiled=True)
    query = jnp.dot(cols, w_query, preferred_element_type=jnp.float32) + b_query
    keyval = jnp.dot(cols, kv_weight, preferred_element_type=jnp.float32) + kv_bias
    return query, keyval


def body_inner(dec_tokens, pre_tokens, w_query, w_keyval, b_query, b_keyval, dec_pool, owner_slots, dec_lengths):
    dec_count = dec_tokens.shape[0]
    q_width = w_query.shape[1]
    kv_width = w_keyval.shape[2]
    kv_weight = w_keyval.reshape(w_keyval.shape[0], 2 * kv_width)
    kv_bias = b_keyval.reshape(2 * kv_width)
    dec_q, dec_kv = project(dec_tokens, w_query, kv_weight, b_query, kv_bias)
    tok_place = lax.axis_index("tok")
    ids = jnp.stack([owner_slots // dec_count, owner_slots % dec_count], axis=1).astype(jnp.bfloat16)
    used = q_width + 2 * kv_width + 2
    pad = jnp.zeros((dec_count, -(-used // 128) * 128 - used), jnp.bfloat16)
    sent = jnp.concatenate([dec_q.astype(jnp.bfloat16), dec_kv.astype(jnp.bfloat16), ids, pad], axis=1)
    got = tree_gather(sent)
    rows = tree_row(tok_place, owner_slots // dec_count, dec_count) + owner_slots % dec_count
    chosen = jnp.take(got, rows, axis=0)
    dec_query = chosen[:, :q_width]
    dec_keyval = chosen[:, q_width:q_width + 2 * kv_width].reshape(dec_count, 2, kv_width)
    served, new_pool = serve_owner(dec_query, dec_keyval, dec_lengths, dec_pool)
    back = tree_gather(served)
    got_ids = got[:, q_width + 2 * kv_width:used].astype(jnp.int32)
    requests = got_ids[:, 0] * dec_count + got_ids[:, 1]
    wanted = tok_place * dec_count + jnp.arange(dec_count, dtype=jnp.int32)
    where = jnp.argmax(requests[None, :] == wanted[:, None], axis=1)
    dec_attn = jnp.take(back, where, axis=0)
    all_query, all_keyval = project(pre_tokens, w_query, kv_weight, b_query, kv_bias)
    return dec_attn, new_pool, all_query, all_keyval


def prefill(all_query, all_keyval, pre_tokens, w_query, w_keyval, pre_cache, pre_offsets):
    pre_count = pre_tokens.shape[0]
    q_width = w_query.shape[1]
    kv_width = w_keyval.shape[2]
    tok_place = lax.axis_index("tok")
    half_id = tok_place % 2
    offset = pre_offsets[tok_place // 2]
    local_pos = jnp.arange(pre_count, dtype=jnp.int32)
    positions = offset + half_id * pre_count + local_pos
    q_heads = q_width // HD
    kv_heads = kv_width // HD
    turned = rotate(all_query.reshape(pre_count, q_heads, HD), positions)
    turned = turned.astype(jnp.bfloat16).reshape(pre_count, q_width)
    pre_kv = all_keyval.reshape(pre_count, 2, kv_width)
    new_keys = rotate(pre_kv[:, 0].reshape(pre_count, kv_heads, HD), positions)
    new_keys = new_keys.astype(jnp.bfloat16).reshape(pre_count, kv_width)
    appended = jnp.stack([new_keys, pre_kv[:, 1].astype(jnp.bfloat16)], axis=0)
    shard = pre_cache.shape[1]
    other_cache, other_new = swapped((pre_cache, appended), "tok", 0)
    is_lower = half_id == 0
    history = jnp.where(
        is_lower,
        jnp.concatenate([pre_cache, other_cache], axis=1),
        jnp.concatenate([other_cache, pre_cache], axis=1),
    )
    block_rows = jnp.where(
        is_lower,
        jnp.concatenate([appended, other_new], axis=1),
        jnp.concatenate([other_new, appended], axis=1),
    )
    key_rows = jnp.concatenate([history, block_rows], axis=1)
    key_slots = jnp.arange(key_rows.shape[1], dtype=jnp.int32)
    key_pos = jnp.where(key_slots < 2 * shard, key_slots, offset + key_slots - 2 * shard)
    usable = (key_slots < offset) | (key_slots >= 2 * shard)
    key_pos = jnp.where(usable, key_pos, jnp.int32(1 << 30))
    return (turned, key_rows[0], key_rows[1], positions, key_pos), appended


def body(dec_tokens, pre_tokens, w_query, w_keyval, b_query, b_keyval, dec_pool, owner_slots, dec_lengths, pre_cache, pre_offsets):
    dec_attn, new_pool, all_query, all_keyval = body_inner(
        dec_tokens, pre_tokens, w_query, w_keyval, b_query, b_keyval, dec_pool, owner_slots, dec_lengths
    )
    operands, appended = prefill(all_query, all_keyval, pre_tokens, w_query, w_keyval, pre_cache, pre_offsets)
    pre_attn = attend(*operands)
    return (dec_attn, pre_attn, new_pool, appended)


def solution(mesh):
    in_specs = (
        P("tok", "kv"),
        P("tok", "kv"),
        P(None, "kv"),
        P(None, None, "kv"),
        P("kv"),
        P(None, "kv"),
        P(None, "tok", "kv"),
        P("tok"),
        P("tok"),
        P(None, "tok", "kv"),
        P(),
    )
    out_specs = (P("tok", "kv"), P("tok", "kv"), P(None, "tok", "kv"), P(None, "tok", "kv"))
    return jax.shard_map(body, mesh=mesh, in_specs=in_specs, out_specs=out_specs, check_vma=False)
```

```python
import jax
import jax.numpy as jnp
from jax import lax
from jax.sharding import PartitionSpec as P
from jax.experimental import pallas as pl

HD = 128


THETA = 1000000.0


def swapped(value, axis, distance):
    return lax.ppermute(value, axis, [(i, i ^ 1 << distance) for i in range(lax.axis_size(axis))])


def rotate(values, positions):
    halfway = values.shape[-1] // 2
    spread = jnp.arange(halfway, dtype=jnp.float32) * (2.0 / values.shape[-1])
    rates = jnp.power(jnp.float32(THETA), -spread)
    angles = positions.astype(jnp.float32)[:, None] * rates[None, :]
    cosine = jnp.cos(angles)[:, None, :]
    sine = jnp.sin(angles)[:, None, :]
    former = values[..., :halfway]
    latter = values[..., halfway:]
    return jnp.concatenate(
        [former * cosine - latter * sine, latter * cosine + former * sine], axis=-1
    )


def attend_kernel(q_ref, k_ref, v_ref, qpos_ref, kpos_ref, o_ref):
    scores = lax.dot_general(
        q_ref[...], k_ref[...], (((1,), (1,)), ((), ())), preferred_element_type=jnp.float32
    ) * HD ** (-0.5)
    allowed = kpos_ref[...] <= qpos_ref[...]
    scores = jnp.where(allowed, scores, -jnp.inf)
    top = jnp.max(scores, axis=1, keepdims=True)
    powers = jnp.exp(scores - top)
    total = jnp.sum(powers, axis=1, keepdims=True)
    mixed = jnp.dot(powers.astype(jnp.bfloat16), v_ref[...], preferred_element_type=jnp.float32)
    o_ref[...] = (mixed / total).astype(o_ref.dtype)


def attend(queries, keys, values, query_pos, key_pos):
    amount, width = queries.shape
    length = keys.shape[0]
    return pl.pallas_call(
        attend_kernel,
        grid=(width // HD,),
        in_specs=[
            pl.BlockSpec((amount, HD), lambda h: (0, h)),
            pl.BlockSpec((length, HD), lambda h: (0, 0)),
            pl.BlockSpec((length, HD), lambda h: (0, 0)),
            pl.BlockSpec((amount, 1), lambda h: (0, 0)),
            pl.BlockSpec((1, length), lambda h: (0, 0)),
        ],
        out_specs=pl.BlockSpec((amount, HD), lambda h: (0, h)),
        out_shape=jax.ShapeDtypeStruct((amount, width), jnp.bfloat16),
    )(queries, keys, values, query_pos.reshape(amount, 1), key_pos.reshape(1, length))


def head_scores(queries, key_rows, allowed):
    amount = queries.shape[0]
    q_heads = queries.shape[1] // HD
    shaped = queries.reshape(amount, q_heads, HD)
    product = jnp.einsum("ngd,md->ngm", shaped, key_rows, preferred_element_type=jnp.float32)
    scores = product * HD ** (-0.5)
    return jnp.where(allowed[:, None, :], scores, -jnp.inf)


def head_mix(scores, peaks, value_rows):
    powers = jnp.exp(scores - peaks[..., None])
    totals = jnp.sum(powers, axis=-1)
    weights = powers.astype(jnp.bfloat16)
    product = jnp.einsum("ngm,md->ngd", weights, value_rows, preferred_element_type=jnp.float32)
    return (totals, product)


def serve_owner(queries, keyval, lengths, cache_pool):
    amount = queries.shape[0]
    q_heads = queries.shape[1] // HD
    kv_heads = cache_pool.shape[2] // HD
    finish = jnp.cumsum(lengths + 1)
    starts = finish - lengths - 1
    turned = rotate(queries.astype(jnp.float32).reshape(amount, q_heads, HD), lengths)
    turned = turned.astype(jnp.bfloat16).reshape(amount, q_heads * HD)
    new_keys = rotate(keyval[:, 0].astype(jnp.float32).reshape(amount, kv_heads, HD), lengths)
    new_keys = new_keys.astype(jnp.bfloat16).reshape(amount, kv_heads * HD)
    appended = jnp.stack([new_keys, keyval[:, 1]], axis=0)
    cache_pool = cache_pool.at[:, starts + lengths].set(appended)
    spots = jnp.arange(cache_pool.shape[1], dtype=jnp.int32)
    allowed = (spots[None, :] >= starts[:, None]) & (spots[None, :] <= (starts + lengths)[:, None])
    scores = head_scores(turned, cache_pool[0], allowed)
    totals, mixed = head_mix(scores, jnp.max(scores, axis=-1), cache_pool[1])
    result = (mixed / totals[..., None]).astype(jnp.bfloat16).reshape(amount, q_heads * HD)
    return (result, cache_pool)


def tree_gather(value):
    buffer = value
    for level, stride, count in (("c", 1, 2), ("y", 2, 4), ("z", 8, 4)):
      parts = [buffer]
      for shift in range(1, count):
          pairs = []
          for i in range(32):
              digit = (i // stride) % count
              target = i + (((digit + shift) % count) - digit) * stride
              pairs.append((i, target))
          parts.append(lax.ppermute(buffer, "tok", pairs))
      if level != "z":
          buffer = jnp.concatenate(parts, axis=0)
    return parts


def pick(parts, rows):
    block = parts[0].shape[0]
    out = None
    for k, part in enumerate(parts):
        got = jnp.take(part, rows % block, axis=0)
        out = got if out is None else jnp.where((rows // block == k)[:, None], got, out)
    return out


def tree_row(place, source, rows):
    core = (place % 2) ^ (source % 2)
    y = ((place // 2) % 4 - (source // 2) % 4) % 4
    z = (place // 8 - source // 8) % 4
    return ((z * 4 + y) * 2 + core) * rows


def project(rows, w_query, kv_weight, b_query, kv_bias):
    cols = lax.all_gather(rows, "kv", axis=1, tiled=True)
    query = jnp.dot(cols, w_query, preferred_element_type=jnp.float32) + b_query
    keyval = jnp.dot(cols, kv_weight, preferred_element_type=jnp.float32) + kv_bias
    return query, keyval


def body_inner(dec_tokens, pre_tokens, w_query, w_keyval, b_query, b_keyval, dec_pool, owner_slots, dec_lengths):
    dec_count = dec_tokens.shape[0]
    q_width = w_query.shape[1]
    kv_width = w_keyval.shape[2]
    kv_weight = w_keyval.reshape(w_keyval.shape[0], 2 * kv_width)
    kv_bias = b_keyval.reshape(2 * kv_width)
    dec_q, dec_kv = project(dec_tokens, w_query, kv_weight, b_query, kv_bias)
    tok_place = lax.axis_index("tok")
    ids = jnp.stack([owner_slots // dec_count, owner_slots % dec_count], axis=1).astype(jnp.bfloat16)
    used = q_width + 2 * kv_width + 2
    pad = jnp.zeros((dec_count, -(-used // 128) * 128 - used), jnp.bfloat16)
    sent = jnp.concatenate([dec_q.astype(jnp.bfloat16), dec_kv.astype(jnp.bfloat16), ids, pad], axis=1)
    got = tree_gather(sent)
    rows = tree_row(tok_place, owner_slots // dec_count, dec_count) + owner_slots % dec_count
    chosen = pick(got, rows)
    dec_query = chosen[:, :q_width]
    dec_keyval = chosen[:, q_width:q_width + 2 * kv_width].reshape(dec_count, 2, kv_width)
    served, new_pool = serve_owner(dec_query, dec_keyval, dec_lengths, dec_pool)
    back = tree_gather(served)
    got_ids = jnp.concatenate([part[:, q_width + 2 * kv_width:used] for part in got], axis=0).astype(jnp.int32)
    requests = got_ids[:, 0] * dec_count + got_ids[:, 1]
    wanted = tok_place * dec_count + jnp.arange(dec_count, dtype=jnp.int32)
    where = jnp.argmax(requests[None, :] == wanted[:, None], axis=1)
    dec_attn = pick(back, where.astype(jnp.int32))
    all_query, all_keyval = project(pre_tokens, w_query, kv_weight, b_query, kv_bias)
    return dec_attn, new_pool, all_query, all_keyval


def prefill(all_query, all_keyval, pre_tokens, w_query, w_keyval, pre_cache, pre_offsets):
    pre_count = pre_tokens.shape[0]
    q_width = w_query.shape[1]
    kv_width = w_keyval.shape[2]
    tok_place = lax.axis_index("tok")
    half_id = tok_place % 2
    offset = pre_offsets[tok_place // 2]
    local_pos = jnp.arange(pre_count, dtype=jnp.int32)
    positions = offset + half_id * pre_count + local_pos
    q_heads = q_width // HD
    kv_heads = kv_width // HD
    turned = rotate(all_query.reshape(pre_count, q_heads, HD), positions)
    turned = turned.astype(jnp.bfloat16).reshape(pre_count, q_width)
    pre_kv = all_keyval.reshape(pre_count, 2, kv_width)
    new_keys = rotate(pre_kv[:, 0].reshape(pre_count, kv_heads, HD), positions)
    new_keys = new_keys.astype(jnp.bfloat16).reshape(pre_count, kv_width)
    appended = jnp.stack([new_keys, pre_kv[:, 1].astype(jnp.bfloat16)], axis=0)
    shard = pre_cache.shape[1]
    other_cache, other_new = swapped((pre_cache, appended), "tok", 0)
    is_lower = half_id == 0
    history = jnp.where(
        is_lower,
        jnp.concatenate([pre_cache, other_cache], axis=1),
        jnp.concatenate([other_cache, pre_cache], axis=1),
    )
    block_rows = jnp.where(
        is_lower,
        jnp.concatenate([appended, other_new], axis=1),
        jnp.concatenate([other_new, appended], axis=1),
    )
    key_rows = jnp.concatenate([history, block_rows], axis=1)
    key_slots = jnp.arange(key_rows.shape[1], dtype=jnp.int32)
    key_pos = jnp.where(key_slots < 2 * shard, key_slots, offset + key_slots - 2 * shard)
    usable = (key_slots < offset) | (key_slots >= 2 * shard)
    key_pos = jnp.where(usable, key_pos, jnp.int32(1 << 30))
    pre_attn = attend(turned, key_rows[0], key_rows[1], positions, key_pos)
    return pre_attn, appended


def body(dec_tokens, pre_tokens, w_query, w_keyval, b_query, b_keyval, dec_pool, owner_slots, dec_lengths, pre_cache, pre_offsets):
    dec_attn, new_pool, all_query, all_keyval = body_inner(
        dec_tokens, pre_tokens, w_query, w_keyval, b_query, b_keyval, dec_pool, owner_slots, dec_lengths
    )
    pre_attn, appended = prefill(all_query, all_keyval, pre_tokens, w_query, w_keyval, pre_cache, pre_offsets)
    return (dec_attn, pre_attn, new_pool, appended)


def solution(mesh):
    in_specs = (
        P("tok", "kv"),
        P("tok", "kv"),
        P(None, "kv"),
        P(None, None, "kv"),
        P("kv"),
        P(None, "kv"),
        P(None, "tok", "kv"),
        P("tok"),
        P("tok"),
        P(None, "tok", "kv"),
        P(),
    )
    out_specs = (P("tok", "kv"), P("tok", "kv"), P(None, "tok", "kv"), P(None, "tok", "kv"))
    return jax.shard_map(body, mesh=mesh, in_specs=in_specs, out_specs=out_specs, check_vma=False)
```

```python
import jax
import jax.numpy as jnp
from jax import lax
from jax.sharding import PartitionSpec as P
from jax.experimental import pallas as pl

HD = 128


THETA = 1000000.0


def swapped(value, axis, distance):
    return lax.ppermute(value, axis, [(i, i ^ 1 << distance) for i in range(lax.axis_size(axis))])


def rotate(values, positions):
    halfway = values.shape[-1] // 2
    spread = jnp.arange(halfway, dtype=jnp.float32) * (2.0 / values.shape[-1])
    rates = jnp.power(jnp.float32(THETA), -spread)
    angles = positions.astype(jnp.float32)[:, None] * rates[None, :]
    cosine = jnp.cos(angles)[:, None, :]
    sine = jnp.sin(angles)[:, None, :]
    former = values[..., :halfway]
    latter = values[..., halfway:]
    return jnp.concatenate(
        [former * cosine - latter * sine, latter * cosine + former * sine], axis=-1
    )


def attend_kernel(q_ref, k_ref, v_ref, qpos_ref, kpos_ref, o_ref):
    scores = lax.dot_general(
        q_ref[...], k_ref[...], (((1,), (1,)), ((), ())), preferred_element_type=jnp.float32
    ) * HD ** (-0.5)
    allowed = kpos_ref[...] <= qpos_ref[...]
    scores = jnp.where(allowed, scores, -jnp.inf)
    top = jnp.max(scores, axis=1, keepdims=True)
    powers = jnp.exp(scores - top)
    total = jnp.sum(powers, axis=1, keepdims=True)
    mixed = jnp.dot(powers.astype(jnp.bfloat16), v_ref[...], preferred_element_type=jnp.float32)
    o_ref[...] = (mixed / total).astype(o_ref.dtype)


def attend(queries, keys, values, query_pos, key_pos):
    amount, width = queries.shape
    length = keys.shape[0]
    return pl.pallas_call(
        attend_kernel,
        grid=(width // HD,),
        in_specs=[
            pl.BlockSpec((amount, HD), lambda h: (0, h)),
            pl.BlockSpec((length, HD), lambda h: (0, 0)),
            pl.BlockSpec((length, HD), lambda h: (0, 0)),
            pl.BlockSpec((amount, 1), lambda h: (0, 0)),
            pl.BlockSpec((1, length), lambda h: (0, 0)),
        ],
        out_specs=pl.BlockSpec((amount, HD), lambda h: (0, h)),
        out_shape=jax.ShapeDtypeStruct((amount, width), jnp.bfloat16),
    )(queries, keys, values, query_pos.reshape(amount, 1), key_pos.reshape(1, length))


def head_scores(queries, key_rows, allowed):
    amount = queries.shape[0]
    q_heads = queries.shape[1] // HD
    shaped = queries.reshape(amount, q_heads, HD)
    product = jnp.einsum("ngd,md->ngm", shaped, key_rows, preferred_element_type=jnp.float32)
    scores = product * HD ** (-0.5)
    return jnp.where(allowed[:, None, :], scores, -jnp.inf)


def head_mix(scores, peaks, value_rows):
    powers = jnp.exp(scores - peaks[..., None])
    totals = jnp.sum(powers, axis=-1)
    weights = powers.astype(jnp.bfloat16)
    product = jnp.einsum("ngm,md->ngd", weights, value_rows, preferred_element_type=jnp.float32)
    return (totals, product)


def serve_owner(queries, keyval, lengths, cache_pool):
    amount = queries.shape[0]
    q_heads = queries.shape[1] // HD
    kv_heads = cache_pool.shape[2] // HD
    finish = jnp.cumsum(lengths + 1)
    starts = finish - lengths - 1
    turned = rotate(queries.astype(jnp.float32).reshape(amount, q_heads, HD), lengths)
    turned = turned.astype(jnp.bfloat16).reshape(amount, q_heads * HD)
    new_keys = rotate(keyval[:, 0].astype(jnp.float32).reshape(amount, kv_heads, HD), lengths)
    new_keys = new_keys.astype(jnp.bfloat16).reshape(amount, kv_heads * HD)
    appended = jnp.stack([new_keys, keyval[:, 1]], axis=0)
    cache_pool = cache_pool.at[:, starts + lengths].set(appended)
    spots = jnp.arange(cache_pool.shape[1], dtype=jnp.int32)
    allowed = (spots[None, :] >= starts[:, None]) & (spots[None, :] <= (starts + lengths)[:, None])
    scores = head_scores(turned, cache_pool[0], allowed)
    totals, mixed = head_mix(scores, jnp.max(scores, axis=-1), cache_pool[1])
    result = (mixed / totals[..., None]).astype(jnp.bfloat16).reshape(amount, q_heads * HD)
    return (result, cache_pool)


def tree_gather(value):
    buffer = value
    for stride, count in ((1, 2), (2, 4), (8, 4)):
      parts = [buffer]
      for shift in range(1, count):
          pairs = []
          for i in range(32):
              digit = (i // stride) % count
              target = i + (((digit + shift) % count) - digit) * stride
              pairs.append((i, target))
          parts.append(lax.ppermute(buffer, "tok", pairs))
      buffer = jnp.concatenate(parts, axis=0)
    return buffer


def tree_row(place, source, rows):
    core = (place % 2) ^ (source % 2)
    y = ((place // 2) % 4 - (source // 2) % 4) % 4
    z = (place // 8 - source // 8) % 4
    return ((z * 4 + y) * 2 + core) * rows


def ring_columns(rows):
    count = lax.axis_size("kv")
    place = lax.axis_index("kv")
    parts = [rows] + [lax.ppermute(rows, "kv", [(i, (i + s) % count) for i in range(count)]) for s in range(1, count)]
    ordered = jnp.take(jnp.stack(parts), (place - jnp.arange(count)) % count, axis=0)
    return jnp.transpose(ordered, (1, 0, 2)).reshape(rows.shape[0], count * rows.shape[1])


def project(rows, w_query, kv_weight, b_query, kv_bias, cols=None):
    if cols is None:
        cols = lax.all_gather(rows, "kv", axis=1, tiled=True)
    query = jnp.dot(cols, w_query, preferred_element_type=jnp.float32) + b_query
    keyval = jnp.dot(cols, kv_weight, preferred_element_type=jnp.float32) + kv_bias
    return query, keyval


def body_inner(dec_tokens, pre_tokens, w_query, w_keyval, b_query, b_keyval, dec_pool, owner_slots, dec_lengths):
    dec_count = dec_tokens.shape[0]
    q_width = w_query.shape[1]
    kv_width = w_keyval.shape[2]
    kv_weight = w_keyval.reshape(w_keyval.shape[0], 2 * kv_width)
    kv_bias = b_keyval.reshape(2 * kv_width)
    pre_cols = ring_columns(pre_tokens)
    dec_q, dec_kv = project(dec_tokens, w_query, kv_weight, b_query, kv_bias)
    tok_place = lax.axis_index("tok")
    ids = jnp.stack([owner_slots // dec_count, owner_slots % dec_count], axis=1).astype(jnp.bfloat16)
    used = q_width + 2 * kv_width + 2
    pad = jnp.zeros((dec_count, -(-used // 128) * 128 - used), jnp.bfloat16)
    sent = jnp.concatenate([dec_q.astype(jnp.bfloat16), dec_kv.astype(jnp.bfloat16), ids, pad], axis=1)
    got = tree_gather(sent)
    rows = tree_row(tok_place, owner_slots // dec_count, dec_count) + owner_slots % dec_count
    chosen = jnp.take(got, rows, axis=0)
    dec_query = chosen[:, :q_width]
    dec_keyval = chosen[:, q_width:q_width + 2 * kv_width].reshape(dec_count, 2, kv_width)
    served, new_pool = serve_owner(dec_query, dec_keyval, dec_lengths, dec_pool)
    back = tree_gather(served)
    got_ids = got[:, q_width + 2 * kv_width:used].astype(jnp.int32)
    requests = got_ids[:, 0] * dec_count + got_ids[:, 1]
    wanted = tok_place * dec_count + jnp.arange(dec_count, dtype=jnp.int32)
    where = jnp.argmax(requests[None, :] == wanted[:, None], axis=1)
    dec_attn = jnp.take(back, where, axis=0)
    all_query, all_keyval = project(pre_tokens, w_query, kv_weight, b_query, kv_bias, cols=pre_cols)
    return dec_attn, new_pool, all_query, all_keyval


def prefill(all_query, all_keyval, pre_tokens, w_query, w_keyval, pre_cache, pre_offsets):
    pre_count = pre_tokens.shape[0]
    q_width = w_query.shape[1]
    kv_width = w_keyval.shape[2]
    tok_place = lax.axis_index("tok")
    half_id = tok_place % 2
    offset = pre_offsets[tok_place // 2]
    local_pos = jnp.arange(pre_count, dtype=jnp.int32)
    positions = offset + half_id * pre_count + local_pos
    q_heads = q_width // HD
    kv_heads = kv_width // HD
    turned = rotate(all_query.reshape(pre_count, q_heads, HD), positions)
    turned = turned.astype(jnp.bfloat16).reshape(pre_count, q_width)
    pre_kv = all_keyval.reshape(pre_count, 2, kv_width)
    new_keys = rotate(pre_kv[:, 0].reshape(pre_count, kv_heads, HD), positions)
    new_keys = new_keys.astype(jnp.bfloat16).reshape(pre_count, kv_width)
    appended = jnp.stack([new_keys, pre_kv[:, 1].astype(jnp.bfloat16)], axis=0)
    shard = pre_cache.shape[1]
    other_cache, other_new = swapped((pre_cache, appended), "tok", 0)
    is_lower = half_id == 0
    history = jnp.where(
        is_lower,
        jnp.concatenate([pre_cache, other_cache], axis=1),
        jnp.concatenate([other_cache, pre_cache], axis=1),
    )
    block_rows = jnp.where(
        is_lower,
        jnp.concatenate([appended, other_new], axis=1),
        jnp.concatenate([other_new, appended], axis=1),
    )
    key_rows = jnp.concatenate([history, block_rows], axis=1)
    key_slots = jnp.arange(key_rows.shape[1], dtype=jnp.int32)
    key_pos = jnp.where(key_slots < 2 * shard, key_slots, offset + key_slots - 2 * shard)
    usable = (key_slots < offset) | (key_slots >= 2 * shard)
    key_pos = jnp.where(usable, key_pos, jnp.int32(1 << 30))
    pre_attn = attend(turned, key_rows[0], key_rows[1], positions, key_pos)
    return pre_attn, appended


def body(dec_tokens, pre_tokens, w_query, w_keyval, b_query, b_keyval, dec_pool, owner_slots, dec_lengths, pre_cache, pre_offsets):
    dec_attn, new_pool, all_query, all_keyval = body_inner(
        dec_tokens, pre_tokens, w_query, w_keyval, b_query, b_keyval, dec_pool, owner_slots, dec_lengths
    )
    pre_attn, appended = prefill(all_query, all_keyval, pre_tokens, w_query, w_keyval, pre_cache, pre_offsets)
    return (dec_attn, pre_attn, new_pool, appended)


def solution(mesh):
    in_specs = (
        P("tok", "kv"),
        P("tok", "kv"),
        P(None, "kv"),
        P(None, None, "kv"),
        P("kv"),
        P(None, "kv"),
        P(None, "tok", "kv"),
        P("tok"),
        P("tok"),
        P(None, "tok", "kv"),
        P(),
    )
    out_specs = (P("tok", "kv"), P("tok", "kv"), P(None, "tok", "kv"), P(None, "tok", "kv"))
    return jax.shard_map(body, mesh=mesh, in_specs=in_specs, out_specs=out_specs, check_vma=False)
```

```python
import jax
import jax.numpy as jnp
from jax import lax
from jax.sharding import PartitionSpec as P
from jax.experimental import pallas as pl

HD = 128


THETA = 1000000.0


def swapped(value, axis, distance):
    return lax.ppermute(value, axis, [(i, i ^ 1 << distance) for i in range(lax.axis_size(axis))])


def rotate(values, positions):
    halfway = values.shape[-1] // 2
    spread = jnp.arange(halfway, dtype=jnp.float32) * (2.0 / values.shape[-1])
    rates = jnp.power(jnp.float32(THETA), -spread)
    angles = positions.astype(jnp.float32)[:, None] * rates[None, :]
    cosine = jnp.cos(angles)[:, None, :]
    sine = jnp.sin(angles)[:, None, :]
    former = values[..., :halfway]
    latter = values[..., halfway:]
    return jnp.concatenate(
        [former * cosine - latter * sine, latter * cosine + former * sine], axis=-1
    )


def attend_kernel(q_ref, k_ref, v_ref, qpos_ref, kpos_ref, o_ref):
    scores = lax.dot_general(
        q_ref[...], k_ref[...], (((1,), (1,)), ((), ())), preferred_element_type=jnp.float32
    ) * HD ** (-0.5)
    allowed = kpos_ref[...] <= qpos_ref[...]
    scores = jnp.where(allowed, scores, -jnp.inf)
    top = jnp.max(scores, axis=1, keepdims=True)
    powers = jnp.exp(scores - top)
    total = jnp.sum(powers, axis=1, keepdims=True)
    mixed = jnp.dot(powers.astype(jnp.bfloat16), v_ref[...], preferred_element_type=jnp.float32)
    o_ref[...] = (mixed / total).astype(o_ref.dtype)


def attend(queries, keys, values, query_pos, key_pos):
    amount, width = queries.shape
    length = keys.shape[0]
    return pl.pallas_call(
        attend_kernel,
        grid=(width // HD,),
        in_specs=[
            pl.BlockSpec((amount, HD), lambda h: (0, h)),
            pl.BlockSpec((length, HD), lambda h: (0, 0)),
            pl.BlockSpec((length, HD), lambda h: (0, 0)),
            pl.BlockSpec((amount, 1), lambda h: (0, 0)),
            pl.BlockSpec((1, length), lambda h: (0, 0)),
        ],
        out_specs=pl.BlockSpec((amount, HD), lambda h: (0, h)),
        out_shape=jax.ShapeDtypeStruct((amount, width), jnp.bfloat16),
    )(queries, keys, values, query_pos.reshape(amount, 1), key_pos.reshape(1, length))


def head_scores(queries, key_rows, allowed):
    amount = queries.shape[0]
    q_heads = queries.shape[1] // HD
    shaped = queries.reshape(amount, q_heads, HD)
    product = jnp.einsum("ngd,md->ngm", shaped, key_rows, preferred_element_type=jnp.float32)
    scores = product * HD ** (-0.5)
    return jnp.where(allowed[:, None, :], scores, -jnp.inf)


def head_mix(scores, peaks, value_rows):
    powers = jnp.exp(scores - peaks[..., None])
    totals = jnp.sum(powers, axis=-1)
    weights = powers.astype(jnp.bfloat16)
    product = jnp.einsum("ngm,md->ngd", weights, value_rows, preferred_element_type=jnp.float32)
    return (totals, product)


def serve_owner(queries, keyval, lengths, cache_pool):
    amount = queries.shape[0]
    q_heads = queries.shape[1] // HD
    kv_heads = cache_pool.shape[2] // HD
    finish = jnp.cumsum(lengths + 1)
    starts = finish - lengths - 1
    turned = rotate(queries.astype(jnp.float32).reshape(amount, q_heads, HD), lengths)
    turned = turned.astype(jnp.bfloat16).reshape(amount, q_heads * HD)
    new_keys = rotate(keyval[:, 0].astype(jnp.float32).reshape(amount, kv_heads, HD), lengths)
    new_keys = new_keys.astype(jnp.bfloat16).reshape(amount, kv_heads * HD)
    appended = jnp.stack([new_keys, keyval[:, 1]], axis=0)
    cache_pool = cache_pool.at[:, starts + lengths].set(appended)
    spots = jnp.arange(cache_pool.shape[1], dtype=jnp.int32)
    allowed = (spots[None, :] >= starts[:, None]) & (spots[None, :] <= (starts + lengths)[:, None])
    scores = head_scores(turned, cache_pool[0], allowed)
    totals, mixed = head_mix(scores, jnp.max(scores, axis=-1), cache_pool[1])
    result = (mixed / totals[..., None]).astype(jnp.bfloat16).reshape(amount, q_heads * HD)
    return (result, cache_pool)


def tree_gather(value):
    buffer = value
    for stride, count in ((1, 2), (2, 4), (8, 4)):
      parts = [buffer]
      for shift in range(1, count):
          pairs = []
          for i in range(32):
              digit = (i // stride) % count
              target = i + (((digit + shift) % count) - digit) * stride
              pairs.append((i, target))
          parts.append(lax.ppermute(buffer, "tok", pairs))
      buffer = jnp.concatenate(parts, axis=0)
    return buffer


def tree_row(place, source, rows):
    core = (place % 2) ^ (source % 2)
    y = ((place // 2) % 4 - (source // 2) % 4) % 4
    z = (place // 8 - source // 8) % 4
    return ((z * 4 + y) * 2 + core) * rows


def ring_parts(rows):
    count = lax.axis_size("kv")
    return [rows] + [lax.ppermute(rows, "kv", [(i, (i + s) % count) for i in range(count)]) for s in range(1, count)]


def ring_project(parts, w_query, kv_weight, b_query, kv_bias):
    count = len(parts)
    width = parts[0].shape[1]

    def branch(place):
        def run(*blocks):
            query = None
            keyval = None
            for shift, block in enumerate(blocks):
                source = (place - shift) % count
                part_q = jnp.dot(block, w_query[source * width:(source + 1) * width], preferred_element_type=jnp.float32)
                part_kv = jnp.dot(block, kv_weight[source * width:(source + 1) * width], preferred_element_type=jnp.float32)
                query = part_q if query is None else query + part_q
                keyval = part_kv if keyval is None else keyval + part_kv
            return query + b_query, keyval + kv_bias

        return run

    return lax.switch(lax.axis_index("kv"), [branch(p) for p in range(count)], *parts)


def project(rows, w_query, kv_weight, b_query, kv_bias, cols=None):
    if cols is None:
        cols = lax.all_gather(rows, "kv", axis=1, tiled=True)
    query = jnp.dot(cols, w_query, preferred_element_type=jnp.float32) + b_query
    keyval = jnp.dot(cols, kv_weight, preferred_element_type=jnp.float32) + kv_bias
    return query, keyval


def body_inner(dec_tokens, pre_tokens, w_query, w_keyval, b_query, b_keyval, dec_pool, owner_slots, dec_lengths):
    dec_count = dec_tokens.shape[0]
    q_width = w_query.shape[1]
    kv_width = w_keyval.shape[2]
    kv_weight = w_keyval.reshape(w_keyval.shape[0], 2 * kv_width)
    kv_bias = b_keyval.reshape(2 * kv_width)
    pre_parts = ring_parts(pre_tokens)
    dec_q, dec_kv = project(dec_tokens, w_query, kv_weight, b_query, kv_bias)
    tok_place = lax.axis_index("tok")
    ids = jnp.stack([owner_slots // dec_count, owner_slots % dec_count], axis=1).astype(jnp.bfloat16)
    used = q_width + 2 * kv_width + 2
    pad = jnp.zeros((dec_count, -(-used // 128) * 128 - used), jnp.bfloat16)
    sent = jnp.concatenate([dec_q.astype(jnp.bfloat16), dec_kv.astype(jnp.bfloat16), ids, pad], axis=1)
    got = tree_gather(sent)
    rows = tree_row(tok_place, owner_slots // dec_count, dec_count) + owner_slots % dec_count
    chosen = jnp.take(got, rows, axis=0)
    dec_query = chosen[:, :q_width]
    dec_keyval = chosen[:, q_width:q_width + 2 * kv_width].reshape(dec_count, 2, kv_width)
    served, new_pool = serve_owner(dec_query, dec_keyval, dec_lengths, dec_pool)
    back = tree_gather(served)
    got_ids = got[:, q_width + 2 * kv_width:used].astype(jnp.int32)
    requests = got_ids[:, 0] * dec_count + got_ids[:, 1]
    wanted = tok_place * dec_count + jnp.arange(dec_count, dtype=jnp.int32)
    where = jnp.argmax(requests[None, :] == wanted[:, None], axis=1)
    dec_attn = jnp.take(back, where, axis=0)
    all_query, all_keyval = ring_project(pre_parts, w_query, kv_weight, b_query, kv_bias)
    return dec_attn, new_pool, all_query, all_keyval


def prefill(all_query, all_keyval, pre_tokens, w_query, w_keyval, pre_cache, pre_offsets):
    pre_count = pre_tokens.shape[0]
    q_width = w_query.shape[1]
    kv_width = w_keyval.shape[2]
    tok_place = lax.axis_index("tok")
    half_id = tok_place % 2
    offset = pre_offsets[tok_place // 2]
    local_pos = jnp.arange(pre_count, dtype=jnp.int32)
    positions = offset + half_id * pre_count + local_pos
    q_heads = q_width // HD
    kv_heads = kv_width // HD
    turned = rotate(all_query.reshape(pre_count, q_heads, HD), positions)
    turned = turned.astype(jnp.bfloat16).reshape(pre_count, q_width)
    pre_kv = all_keyval.reshape(pre_count, 2, kv_width)
    new_keys = rotate(pre_kv[:, 0].reshape(pre_count, kv_heads, HD), positions)
    new_keys = new_keys.astype(jnp.bfloat16).reshape(pre_count, kv_width)
    appended = jnp.stack([new_keys, pre_kv[:, 1].astype(jnp.bfloat16)], axis=0)
    shard = pre_cache.shape[1]
    other_cache, other_new = swapped((pre_cache, appended), "tok", 0)
    is_lower = half_id == 0
    history = jnp.where(
        is_lower,
        jnp.concatenate([pre_cache, other_cache], axis=1),
        jnp.concatenate([other_cache, pre_cache], axis=1),
    )
    block_rows = jnp.where(
        is_lower,
        jnp.concatenate([appended, other_new], axis=1),
        jnp.concatenate([other_new, appended], axis=1),
    )
    key_rows = jnp.concatenate([history, block_rows], axis=1)
    key_slots = jnp.arange(key_rows.shape[1], dtype=jnp.int32)
    key_pos = jnp.where(key_slots < 2 * shard, key_slots, offset + key_slots - 2 * shard)
    usable = (key_slots < offset) | (key_slots >= 2 * shard)
    key_pos = jnp.where(usable, key_pos, jnp.int32(1 << 30))
    pre_attn = attend(turned, key_rows[0], key_rows[1], positions, key_pos)
    return pre_attn, appended


def body(dec_tokens, pre_tokens, w_query, w_keyval, b_query, b_keyval, dec_pool, owner_slots, dec_lengths, pre_cache, pre_offsets):
    dec_attn, new_pool, all_query, all_keyval = body_inner(
        dec_tokens, pre_tokens, w_query, w_keyval, b_query, b_keyval, dec_pool, owner_slots, dec_lengths
    )
    pre_attn, appended = prefill(all_query, all_keyval, pre_tokens, w_query, w_keyval, pre_cache, pre_offsets)
    return (dec_attn, pre_attn, new_pool, appended)


def solution(mesh):
    in_specs = (
        P("tok", "kv"),
        P("tok", "kv"),
        P(None, "kv"),
        P(None, None, "kv"),
        P("kv"),
        P(None, "kv"),
        P(None, "tok", "kv"),
        P("tok"),
        P("tok"),
        P(None, "tok", "kv"),
        P(),
    )
    out_specs = (P("tok", "kv"), P("tok", "kv"), P(None, "tok", "kv"), P(None, "tok", "kv"))
    return jax.shard_map(body, mesh=mesh, in_specs=in_specs, out_specs=out_specs, check_vma=False)
```

```python
import jax
import jax.numpy as jnp
from jax import lax
from jax.sharding import PartitionSpec as P
from jax.experimental import pallas as pl

HD = 128


THETA = 1000000.0


def swapped(value, axis, distance):
    return lax.ppermute(value, axis, [(i, i ^ 1 << distance) for i in range(lax.axis_size(axis))])


def rotate(values, positions):
    halfway = values.shape[-1] // 2
    spread = jnp.arange(halfway, dtype=jnp.float32) * (2.0 / values.shape[-1])
    rates = jnp.power(jnp.float32(THETA), -spread)
    angles = positions.astype(jnp.float32)[:, None] * rates[None, :]
    cosine = jnp.cos(angles)[:, None, :]
    sine = jnp.sin(angles)[:, None, :]
    former = values[..., :halfway]
    latter = values[..., halfway:]
    return jnp.concatenate(
        [former * cosine - latter * sine, latter * cosine + former * sine], axis=-1
    )


def attend_kernel(q_ref, k_ref, v_ref, qpos_ref, kpos_ref, o_ref):
    scores = lax.dot_general(
        q_ref[...], k_ref[...], (((1,), (1,)), ((), ())), preferred_element_type=jnp.float32
    ) * HD ** (-0.5)
    allowed = kpos_ref[...] <= qpos_ref[...]
    scores = jnp.where(allowed, scores, -jnp.inf)
    top = jnp.max(scores, axis=1, keepdims=True)
    powers = jnp.exp(scores - top)
    total = jnp.sum(powers, axis=1, keepdims=True)
    mixed = jnp.dot(powers.astype(jnp.bfloat16), v_ref[...], preferred_element_type=jnp.float32)
    o_ref[...] = (mixed / total).astype(o_ref.dtype)


def attend(queries, keys, values, query_pos, key_pos):
    amount, width = queries.shape
    length = keys.shape[0]
    return pl.pallas_call(
        attend_kernel,
        grid=(width // HD,),
        in_specs=[
            pl.BlockSpec((amount, HD), lambda h: (0, h)),
            pl.BlockSpec((length, HD), lambda h: (0, 0)),
            pl.BlockSpec((length, HD), lambda h: (0, 0)),
            pl.BlockSpec((amount, 1), lambda h: (0, 0)),
            pl.BlockSpec((1, length), lambda h: (0, 0)),
        ],
        out_specs=pl.BlockSpec((amount, HD), lambda h: (0, h)),
        out_shape=jax.ShapeDtypeStruct((amount, width), jnp.bfloat16),
    )(queries, keys, values, query_pos.reshape(amount, 1), key_pos.reshape(1, length))


def head_scores(queries, key_rows, allowed):
    amount = queries.shape[0]
    q_heads = queries.shape[1] // HD
    shaped = queries.reshape(amount, q_heads, HD)
    product = jnp.einsum("ngd,md->ngm", shaped, key_rows, preferred_element_type=jnp.float32)
    scores = product * HD ** (-0.5)
    return jnp.where(allowed[:, None, :], scores, -jnp.inf)


def head_mix(scores, peaks, value_rows):
    powers = jnp.exp(scores - peaks[..., None])
    totals = jnp.sum(powers, axis=-1)
    weights = powers.astype(jnp.bfloat16)
    product = jnp.einsum("ngm,md->ngd", weights, value_rows, preferred_element_type=jnp.float32)
    return (totals, product)


def serve_owner(queries, keyval, lengths, cache_pool):
    amount = queries.shape[0]
    q_heads = queries.shape[1] // HD
    kv_heads = cache_pool.shape[2] // HD
    finish = jnp.cumsum(lengths + 1)
    starts = finish - lengths - 1
    turned = rotate(queries.astype(jnp.float32).reshape(amount, q_heads, HD), lengths)
    turned = turned.astype(jnp.bfloat16).reshape(amount, q_heads * HD)
    new_keys = rotate(keyval[:, 0].astype(jnp.float32).reshape(amount, kv_heads, HD), lengths)
    new_keys = new_keys.astype(jnp.bfloat16).reshape(amount, kv_heads * HD)
    appended = jnp.stack([new_keys, keyval[:, 1]], axis=0)
    cache_pool = cache_pool.at[:, starts + lengths].set(appended)
    spots = jnp.arange(cache_pool.shape[1], dtype=jnp.int32)
    allowed = (spots[None, :] >= starts[:, None]) & (spots[None, :] <= (starts + lengths)[:, None])
    scores = head_scores(turned, cache_pool[0], allowed)
    totals, mixed = head_mix(scores, jnp.max(scores, axis=-1), cache_pool[1])
    result = (mixed / totals[..., None]).astype(jnp.bfloat16).reshape(amount, q_heads * HD)
    return (result, cache_pool)


def tree_gather(value):
    buffer = value
    for stride, count in ((1, 2), (2, 4), (8, 4)):
      parts = [buffer]
      for shift in range(1, count):
          pairs = []
          for i in range(32):
              digit = (i // stride) % count
              target = i + (((digit + shift) % count) - digit) * stride
              pairs.append((i, target))
          parts.append(lax.ppermute(buffer, "tok", pairs))
      buffer = jnp.concatenate(parts, axis=0)
    return buffer


def tree_row(place, source, rows):
    core = (place % 2) ^ (source % 2)
    y = ((place // 2) % 4 - (source // 2) % 4) % 4
    z = (place // 8 - source // 8) % 4
    return ((z * 4 + y) * 2 + core) * rows


def swap_columns(rows):
    count = lax.axis_size("kv")
    tiled = jnp.broadcast_to(rows[None], (count,) + rows.shape)
    blocks = lax.all_to_all(tiled, "kv", 0, 0, tiled=False)
    return jnp.transpose(blocks, (1, 0, 2)).reshape(rows.shape[0], count * rows.shape[1])


def project(rows, w_query, kv_weight, b_query, kv_bias, small=False):
    cols = swap_columns(rows) if small else lax.all_gather(rows, "kv", axis=1, tiled=True)
    query = jnp.dot(cols, w_query, preferred_element_type=jnp.float32) + b_query
    keyval = jnp.dot(cols, kv_weight, preferred_element_type=jnp.float32) + kv_bias
    return query, keyval


def body_inner(dec_tokens, pre_tokens, w_query, w_keyval, b_query, b_keyval, dec_pool, owner_slots, dec_lengths):
    dec_count = dec_tokens.shape[0]
    q_width = w_query.shape[1]
    kv_width = w_keyval.shape[2]
    kv_weight = w_keyval.reshape(w_keyval.shape[0], 2 * kv_width)
    kv_bias = b_keyval.reshape(2 * kv_width)
    dec_q, dec_kv = project(dec_tokens, w_query, kv_weight, b_query, kv_bias, small=True)
    tok_place = lax.axis_index("tok")
    ids = jnp.stack([owner_slots // dec_count, owner_slots % dec_count], axis=1).astype(jnp.bfloat16)
    used = q_width + 2 * kv_width + 2
    pad = jnp.zeros((dec_count, -(-used // 128) * 128 - used), jnp.bfloat16)
    sent = jnp.concatenate([dec_q.astype(jnp.bfloat16), dec_kv.astype(jnp.bfloat16), ids, pad], axis=1)
    got = tree_gather(sent)
    rows = tree_row(tok_place, owner_slots // dec_count, dec_count) + owner_slots % dec_count
    chosen = jnp.take(got, rows, axis=0)
    dec_query = chosen[:, :q_width]
    dec_keyval = chosen[:, q_width:q_width + 2 * kv_width].reshape(dec_count, 2, kv_width)
    served, new_pool = serve_owner(dec_query, dec_keyval, dec_lengths, dec_pool)
    back = tree_gather(served)
    got_ids = got[:, q_width + 2 * kv_width:used].astype(jnp.int32)
    requests = got_ids[:, 0] * dec_count + got_ids[:, 1]
    wanted = tok_place * dec_count + jnp.arange(dec_count, dtype=jnp.int32)
    where = jnp.argmax(requests[None, :] == wanted[:, None], axis=1)
    dec_attn = jnp.take(back, where, axis=0)
    all_query, all_keyval = project(pre_tokens, w_query, kv_weight, b_query, kv_bias)
    return dec_attn, new_pool, all_query, all_keyval


def prefill(all_query, all_keyval, pre_tokens, w_query, w_keyval, pre_cache, pre_offsets):
    pre_count = pre_tokens.shape[0]
    q_width = w_query.shape[1]
    kv_width = w_keyval.shape[2]
    tok_place = lax.axis_index("tok")
    half_id = tok_place % 2
    offset = pre_offsets[tok_place // 2]
    local_pos = jnp.arange(pre_count, dtype=jnp.int32)
    positions = offset + half_id * pre_count + local_pos
    q_heads = q_width // HD
    kv_heads = kv_width // HD
    turned = rotate(all_query.reshape(pre_count, q_heads, HD), positions)
    turned = turned.astype(jnp.bfloat16).reshape(pre_count, q_width)
    pre_kv = all_keyval.reshape(pre_count, 2, kv_width)
    new_keys = rotate(pre_kv[:, 0].reshape(pre_count, kv_heads, HD), positions)
    new_keys = new_keys.astype(jnp.bfloat16).reshape(pre_count, kv_width)
    appended = jnp.stack([new_keys, pre_kv[:, 1].astype(jnp.bfloat16)], axis=0)
    shard = pre_cache.shape[1]
    other_cache, other_new = swapped((pre_cache, appended), "tok", 0)
    is_lower = half_id == 0
    history = jnp.where(
        is_lower,
        jnp.concatenate([pre_cache, other_cache], axis=1),
        jnp.concatenate([other_cache, pre_cache], axis=1),
    )
    block_rows = jnp.where(
        is_lower,
        jnp.concatenate([appended, other_new], axis=1),
        jnp.concatenate([other_new, appended], axis=1),
    )
    key_rows = jnp.concatenate([history, block_rows], axis=1)
    key_slots = jnp.arange(key_rows.shape[1], dtype=jnp.int32)
    key_pos = jnp.where(key_slots < 2 * shard, key_slots, offset + key_slots - 2 * shard)
    usable = (key_slots < offset) | (key_slots >= 2 * shard)
    key_pos = jnp.where(usable, key_pos, jnp.int32(1 << 30))
    return (turned, key_rows[0], key_rows[1], positions, key_pos), appended


def body(dec_tokens, pre_tokens, w_query, w_keyval, b_query, b_keyval, dec_pool, owner_slots, dec_lengths, pre_cache, pre_offsets):
    dec_attn, new_pool, all_query, all_keyval = body_inner(
        dec_tokens, pre_tokens, w_query, w_keyval, b_query, b_keyval, dec_pool, owner_slots, dec_lengths
    )
    operands, appended = prefill(all_query, all_keyval, pre_tokens, w_query, w_keyval, pre_cache, pre_offsets)
    pre_attn = attend(*operands)
    return (dec_attn, pre_attn, new_pool, appended)


def solution(mesh):
    in_specs = (
        P("tok", "kv"),
        P("tok", "kv"),
        P(None, "kv"),
        P(None, None, "kv"),
        P("kv"),
        P(None, "kv"),
        P(None, "tok", "kv"),
        P("tok"),
        P("tok"),
        P(None, "tok", "kv"),
        P(),
    )
    out_specs = (P("tok", "kv"), P("tok", "kv"), P(None, "tok", "kv"), P(None, "tok", "kv"))
    return jax.shard_map(body, mesh=mesh, in_specs=in_specs, out_specs=out_specs, check_vma=False)
```

```python
import jax
import jax.numpy as jnp
from jax import lax
from jax.sharding import PartitionSpec as P
from jax.experimental import pallas as pl

HD = 128


THETA = 1000000.0


def swapped(value, axis, distance):
    return lax.ppermute(value, axis, [(i, i ^ 1 << distance) for i in range(lax.axis_size(axis))])


def rotate(values, positions):
    halfway = values.shape[-1] // 2
    spread = jnp.arange(halfway, dtype=jnp.float32) * (2.0 / values.shape[-1])
    rates = jnp.power(jnp.float32(THETA), -spread)
    angles = positions.astype(jnp.float32)[:, None] * rates[None, :]
    cosine = jnp.cos(angles)[:, None, :]
    sine = jnp.sin(angles)[:, None, :]
    former = values[..., :halfway]
    latter = values[..., halfway:]
    return jnp.concatenate(
        [former * cosine - latter * sine, latter * cosine + former * sine], axis=-1
    )


def attend_kernel(q_ref, k_ref, v_ref, qpos_ref, kpos_ref, o_ref):
    scores = lax.dot_general(
        q_ref[...], k_ref[...], (((1,), (1,)), ((), ())), preferred_element_type=jnp.float32
    ) * HD ** (-0.5)
    allowed = kpos_ref[...] <= qpos_ref[...]
    scores = jnp.where(allowed, scores, -jnp.inf)
    top = jnp.max(scores, axis=1, keepdims=True)
    powers = jnp.exp(scores - top)
    total = jnp.sum(powers, axis=1, keepdims=True)
    mixed = jnp.dot(powers.astype(jnp.bfloat16), v_ref[...], preferred_element_type=jnp.float32)
    o_ref[...] = (mixed / total).astype(o_ref.dtype)


def attend(queries, keys, values, query_pos, key_pos):
    amount, width = queries.shape
    length = keys.shape[0]
    return pl.pallas_call(
        attend_kernel,
        grid=(width // HD,),
        in_specs=[
            pl.BlockSpec((amount, HD), lambda h: (0, h)),
            pl.BlockSpec((length, HD), lambda h: (0, 0)),
            pl.BlockSpec((length, HD), lambda h: (0, 0)),
            pl.BlockSpec((amount, 1), lambda h: (0, 0)),
            pl.BlockSpec((1, length), lambda h: (0, 0)),
        ],
        out_specs=pl.BlockSpec((amount, HD), lambda h: (0, h)),
        out_shape=jax.ShapeDtypeStruct((amount, width), jnp.bfloat16),
    )(queries, keys, values, query_pos.reshape(amount, 1), key_pos.reshape(1, length))


def head_scores(queries, key_rows, allowed):
    amount = queries.shape[0]
    q_heads = queries.shape[1] // HD
    shaped = queries.reshape(amount, q_heads, HD)
    product = jnp.einsum("ngd,md->ngm", shaped, key_rows, preferred_element_type=jnp.float32)
    scores = product * HD ** (-0.5)
    return jnp.where(allowed[:, None, :], scores, -jnp.inf)


def head_mix(scores, peaks, value_rows):
    powers = jnp.exp(scores - peaks[..., None])
    totals = jnp.sum(powers, axis=-1)
    weights = powers.astype(jnp.bfloat16)
    product = jnp.einsum("ngm,md->ngd", weights, value_rows, preferred_element_type=jnp.float32)
    return (totals, product)


def serve_owner(queries, keyval, lengths, cache_pool):
    amount = queries.shape[0]
    q_heads = queries.shape[1] // HD
    kv_heads = cache_pool.shape[2] // HD
    finish = jnp.cumsum(lengths + 1)
    starts = finish - lengths - 1
    turned = rotate(queries.astype(jnp.float32).reshape(amount, q_heads, HD), lengths)
    turned = turned.astype(jnp.bfloat16).reshape(amount, q_heads * HD)
    new_keys = rotate(keyval[:, 0].astype(jnp.float32).reshape(amount, kv_heads, HD), lengths)
    new_keys = new_keys.astype(jnp.bfloat16).reshape(amount, kv_heads * HD)
    appended = jnp.stack([new_keys, keyval[:, 1]], axis=0)
    cache_pool = cache_pool.at[:, starts + lengths].set(appended)
    spots = jnp.arange(cache_pool.shape[1], dtype=jnp.int32)
    allowed = (spots[None, :] >= starts[:, None]) & (spots[None, :] <= (starts + lengths)[:, None])
    scores = head_scores(turned, cache_pool[0], allowed)
    totals, mixed = head_mix(scores, jnp.max(scores, axis=-1), cache_pool[1])
    result = (mixed / totals[..., None]).astype(jnp.bfloat16).reshape(amount, q_heads * HD)
    return (result, cache_pool)


def tree_gather(value):
    buffer = value
    for stride, count in ((1, 2), (2, 4), (8, 4)):
      parts = [buffer]
      for shift in range(1, count):
          pairs = []
          for i in range(32):
              digit = (i // stride) % count
              target = i + (((digit + shift) % count) - digit) * stride
              pairs.append((i, target))
          parts.append(lax.ppermute(buffer, "tok", pairs))
      buffer = jnp.concatenate(parts, axis=0)
    return buffer


def tree_row(place, source, rows):
    core = (place % 2) ^ (source % 2)
    y = ((place // 2) % 4 - (source // 2) % 4) % 4
    z = (place // 8 - source // 8) % 4
    return ((z * 4 + y) * 2 + core) * rows


def swap_columns(rows):
    count = lax.axis_size("kv")
    tiled = jnp.broadcast_to(rows[None], (count,) + rows.shape)
    blocks = lax.all_to_all(tiled, "kv", 0, 0, tiled=False)
    return jnp.transpose(blocks, (1, 0, 2)).reshape(rows.shape[0], count * rows.shape[1])


def block_project(rows, after, w_query, kv_weight, b_query, kv_bias):
    count = lax.axis_size("kv")
    width = rows.shape[1]
    tiled = jnp.broadcast_to(rows[None], (count,) + rows.shape)
    tiled, after = lax.optimization_barrier((tiled, after))
    blocks = lax.all_to_all(tiled, "kv", 0, 0, tiled=False)
    query = None
    keyval = None
    for source in range(count):
        part_q = jnp.dot(blocks[source], w_query[source * width:(source + 1) * width], preferred_element_type=jnp.float32)
        part_kv = jnp.dot(blocks[source], kv_weight[source * width:(source + 1) * width], preferred_element_type=jnp.float32)
        query = part_q if query is None else query + part_q
        keyval = part_kv if keyval is None else keyval + part_kv
    return query + b_query, keyval + kv_bias, after


def body_inner(dec_tokens, pre_tokens, w_query, w_keyval, b_query, b_keyval, dec_pool, owner_slots, dec_lengths):
    dec_count = dec_tokens.shape[0]
    q_width = w_query.shape[1]
    kv_width = w_keyval.shape[2]
    kv_weight = w_keyval.reshape(w_keyval.shape[0], 2 * kv_width)
    kv_bias = b_keyval.reshape(2 * kv_width)
    dec_cols = swap_columns(dec_tokens)
    pre_q, pre_kv, dec_cols = block_project(pre_tokens, dec_cols, w_query, kv_weight, b_query, kv_bias)
    dec_q = jnp.dot(dec_cols, w_query, preferred_element_type=jnp.float32) + b_query
    dec_kv = jnp.dot(dec_cols, kv_weight, preferred_element_type=jnp.float32) + kv_bias
    tok_place = lax.axis_index("tok")
    ids = jnp.stack([owner_slots // dec_count, owner_slots % dec_count], axis=1).astype(jnp.bfloat16)
    used = q_width + 2 * kv_width + 2
    pad = jnp.zeros((dec_count, -(-used // 128) * 128 - used), jnp.bfloat16)
    sent = jnp.concatenate([dec_q.astype(jnp.bfloat16), dec_kv.astype(jnp.bfloat16), ids, pad], axis=1)
    got = tree_gather(sent)
    rows = tree_row(tok_place, owner_slots // dec_count, dec_count) + owner_slots % dec_count
    chosen = jnp.take(got, rows, axis=0)
    dec_query = chosen[:, :q_width]
    dec_keyval = chosen[:, q_width:q_width + 2 * kv_width].reshape(dec_count, 2, kv_width)
    served, new_pool = serve_owner(dec_query, dec_keyval, dec_lengths, dec_pool)
    back = tree_gather(served)
    got_ids = got[:, q_width + 2 * kv_width:used].astype(jnp.int32)
    requests = got_ids[:, 0] * dec_count + got_ids[:, 1]
    wanted = tok_place * dec_count + jnp.arange(dec_count, dtype=jnp.int32)
    where = jnp.argmax(requests[None, :] == wanted[:, None], axis=1)
    dec_attn = jnp.take(back, where, axis=0)
    all_query, all_keyval = pre_q, pre_kv
    return dec_attn, new_pool, all_query, all_keyval


def prefill(all_query, all_keyval, pre_tokens, w_query, w_keyval, pre_cache, pre_offsets):
    pre_count = pre_tokens.shape[0]
    q_width = w_query.shape[1]
    kv_width = w_keyval.shape[2]
    tok_place = lax.axis_index("tok")
    half_id = tok_place % 2
    offset = pre_offsets[tok_place // 2]
    local_pos = jnp.arange(pre_count, dtype=jnp.int32)
    positions = offset + half_id * pre_count + local_pos
    q_heads = q_width // HD
    kv_heads = kv_width // HD
    turned = rotate(all_query.reshape(pre_count, q_heads, HD), positions)
    turned = turned.astype(jnp.bfloat16).reshape(pre_count, q_width)
    pre_kv = all_keyval.reshape(pre_count, 2, kv_width)
    new_keys = rotate(pre_kv[:, 0].reshape(pre_count, kv_heads, HD), positions)
    new_keys = new_keys.astype(jnp.bfloat16).reshape(pre_count, kv_width)
    appended = jnp.stack([new_keys, pre_kv[:, 1].astype(jnp.bfloat16)], axis=0)
    shard = pre_cache.shape[1]
    other_cache, other_new = swapped((pre_cache, appended), "tok", 0)
    is_lower = half_id == 0
    history = jnp.where(
        is_lower,
        jnp.concatenate([pre_cache, other_cache], axis=1),
        jnp.concatenate([other_cache, pre_cache], axis=1),
    )
    block_rows = jnp.where(
        is_lower,
        jnp.concatenate([appended, other_new], axis=1),
        jnp.concatenate([other_new, appended], axis=1),
    )
    key_rows = jnp.concatenate([history, block_rows], axis=1)
    key_slots = jnp.arange(key_rows.shape[1], dtype=jnp.int32)
    key_pos = jnp.where(key_slots < 2 * shard, key_slots, offset + key_slots - 2 * shard)
    usable = (key_slots < offset) | (key_slots >= 2 * shard)
    key_pos = jnp.where(usable, key_pos, jnp.int32(1 << 30))
    return (turned, key_rows[0], key_rows[1], positions, key_pos), appended


def body(dec_tokens, pre_tokens, w_query, w_keyval, b_query, b_keyval, dec_pool, owner_slots, dec_lengths, pre_cache, pre_offsets):
    dec_attn, new_pool, all_query, all_keyval = body_inner(
        dec_tokens, pre_tokens, w_query, w_keyval, b_query, b_keyval, dec_pool, owner_slots, dec_lengths
    )
    operands, appended = prefill(all_query, all_keyval, pre_tokens, w_query, w_keyval, pre_cache, pre_offsets)
    pre_attn = attend(*operands)
    return (dec_attn, pre_attn, new_pool, appended)


def solution(mesh):
    in_specs = (
        P("tok", "kv"),
        P("tok", "kv"),
        P(None, "kv"),
        P(None, None, "kv"),
        P("kv"),
        P(None, "kv"),
        P(None, "tok", "kv"),
        P("tok"),
        P("tok"),
        P(None, "tok", "kv"),
        P(),
    )
    out_specs = (P("tok", "kv"), P("tok", "kv"), P(None, "tok", "kv"), P(None, "tok", "kv"))
    return jax.shard_map(body, mesh=mesh, in_specs=in_specs, out_specs=out_specs, check_vma=False)
```

```python
import jax
import jax.numpy as jnp
from jax import lax
from jax.sharding import PartitionSpec as P
from jax.experimental import pallas as pl

HD = 128


THETA = 1000000.0


def swapped(value, axis, distance):
    return lax.ppermute(value, axis, [(i, i ^ 1 << distance) for i in range(lax.axis_size(axis))])


def rotate(values, positions):
    halfway = values.shape[-1] // 2
    spread = jnp.arange(halfway, dtype=jnp.float32) * (2.0 / values.shape[-1])
    rates = jnp.power(jnp.float32(THETA), -spread)
    angles = positions.astype(jnp.float32)[:, None] * rates[None, :]
    cosine = jnp.cos(angles)[:, None, :]
    sine = jnp.sin(angles)[:, None, :]
    former = values[..., :halfway]
    latter = values[..., halfway:]
    return jnp.concatenate(
        [former * cosine - latter * sine, latter * cosine + former * sine], axis=-1
    )


def attend_kernel(q_ref, k_ref, v_ref, qpos_ref, kpos_ref, o_ref):
    scores = lax.dot_general(
        q_ref[...], k_ref[...], (((1,), (1,)), ((), ())), preferred_element_type=jnp.float32
    ) * HD ** (-0.5)
    allowed = kpos_ref[...] <= qpos_ref[...]
    scores = jnp.where(allowed, scores, -jnp.inf)
    top = jnp.max(scores, axis=1, keepdims=True)
    powers = jnp.exp(scores - top)
    total = jnp.sum(powers, axis=1, keepdims=True)
    mixed = jnp.dot(powers.astype(jnp.bfloat16), v_ref[...], preferred_element_type=jnp.float32)
    o_ref[...] = (mixed / total).astype(o_ref.dtype)


def attend(queries, keys, values, query_pos, key_pos):
    amount, width = queries.shape
    length = keys.shape[0]
    return pl.pallas_call(
        attend_kernel,
        grid=(width // HD,),
        in_specs=[
            pl.BlockSpec((amount, HD), lambda h: (0, h)),
            pl.BlockSpec((length, HD), lambda h: (0, 0)),
            pl.BlockSpec((length, HD), lambda h: (0, 0)),
            pl.BlockSpec((amount, 1), lambda h: (0, 0)),
            pl.BlockSpec((1, length), lambda h: (0, 0)),
        ],
        out_specs=pl.BlockSpec((amount, HD), lambda h: (0, h)),
        out_shape=jax.ShapeDtypeStruct((amount, width), jnp.bfloat16),
    )(queries, keys, values, query_pos.reshape(amount, 1), key_pos.reshape(1, length))


def head_scores(queries, key_rows, allowed):
    amount = queries.shape[0]
    q_heads = queries.shape[1] // HD
    shaped = queries.reshape(amount, q_heads, HD)
    product = jnp.einsum("ngd,md->ngm", shaped, key_rows, preferred_element_type=jnp.float32)
    scores = product * HD ** (-0.5)
    return jnp.where(allowed[:, None, :], scores, -jnp.inf)


def head_mix(scores, peaks, value_rows):
    powers = jnp.exp(scores - peaks[..., None])
    totals = jnp.sum(powers, axis=-1)
    weights = powers.astype(jnp.bfloat16)
    product = jnp.einsum("ngm,md->ngd", weights, value_rows, preferred_element_type=jnp.float32)
    return (totals, product)


def serve_owner(queries, keyval, lengths, cache_pool):
    amount = queries.shape[0]
    q_heads = queries.shape[1] // HD
    kv_heads = cache_pool.shape[2] // HD
    finish = jnp.cumsum(lengths + 1)
    starts = finish - lengths - 1
    turned = rotate(queries.astype(jnp.float32).reshape(amount, q_heads, HD), lengths)
    turned = turned.astype(jnp.bfloat16).reshape(amount, q_heads * HD)
    new_keys = rotate(keyval[:, 0].astype(jnp.float32).reshape(amount, kv_heads, HD), lengths)
    new_keys = new_keys.astype(jnp.bfloat16).reshape(amount, kv_heads * HD)
    appended = jnp.stack([new_keys, keyval[:, 1]], axis=0)
    cache_pool = cache_pool.at[:, starts + lengths].set(appended)
    spots = jnp.arange(cache_pool.shape[1], dtype=jnp.int32)
    allowed = (spots[None, :] >= starts[:, None]) & (spots[None, :] <= (starts + lengths)[:, None])
    scores = head_scores(turned, cache_pool[0], allowed)
    totals, mixed = head_mix(scores, jnp.max(scores, axis=-1), cache_pool[1])
    result = (mixed / totals[..., None]).astype(jnp.bfloat16).reshape(amount, q_heads * HD)
    return (result, cache_pool)


def tree_gather(value):
    buffer = value
    for stride, count in ((1, 2), (2, 4), (8, 4)):
      parts = [buffer]
      for shift in range(1, count):
          pairs = []
          for i in range(32):
              digit = (i // stride) % count
              target = i + (((digit + shift) % count) - digit) * stride
              pairs.append((i, target))
          parts.append(lax.ppermute(buffer, "tok", pairs))
      buffer = jnp.concatenate(parts, axis=0)
    return buffer


def tree_row(place, source, rows):
    core = (place % 2) ^ (source % 2)
    y = ((place // 2) % 4 - (source // 2) % 4) % 4
    z = (place // 8 - source // 8) % 4
    return ((z * 4 + y) * 2 + core) * rows


def swap_columns(rows):
    count = lax.axis_size("kv")
    tiled = jnp.broadcast_to(rows[None], (count,) + rows.shape)
    blocks = lax.all_to_all(tiled, "kv", 0, 0, tiled=False)
    return jnp.transpose(blocks, (1, 0, 2)).reshape(rows.shape[0], count * rows.shape[1])


def block_project(rows, after, w_query, kv_weight, b_query, kv_bias):
    count = lax.axis_size("kv")
    width = rows.shape[1]
    tiled = jnp.broadcast_to(rows[None], (count,) + rows.shape)
    tiled, after = lax.optimization_barrier((tiled, after))
    blocks = lax.all_to_all(tiled, "kv", 0, 0, tiled=False)
    cols = jnp.transpose(blocks, (1, 0, 2)).reshape(rows.shape[0], count * width)
    query = jnp.dot(cols, w_query, preferred_element_type=jnp.float32) + b_query
    keyval = jnp.dot(cols, kv_weight, preferred_element_type=jnp.float32) + kv_bias
    return query, keyval, after


def body_inner(dec_tokens, pre_tokens, w_query, w_keyval, b_query, b_keyval, dec_pool, owner_slots, dec_lengths):
    dec_count = dec_tokens.shape[0]
    q_width = w_query.shape[1]
    kv_width = w_keyval.shape[2]
    kv_weight = w_keyval.reshape(w_keyval.shape[0], 2 * kv_width)
    kv_bias = b_keyval.reshape(2 * kv_width)
    dec_cols = swap_columns(dec_tokens)
    pre_q, pre_kv, dec_cols = block_project(pre_tokens, dec_cols, w_query, kv_weight, b_query, kv_bias)
    dec_q = jnp.dot(dec_cols, w_query, preferred_element_type=jnp.float32) + b_query
    dec_kv = jnp.dot(dec_cols, kv_weight, preferred_element_type=jnp.float32) + kv_bias
    tok_place = lax.axis_index("tok")
    ids = jnp.stack([owner_slots // dec_count, owner_slots % dec_count], axis=1).astype(jnp.bfloat16)
    used = q_width + 2 * kv_width + 2
    pad = jnp.zeros((dec_count, -(-used // 128) * 128 - used), jnp.bfloat16)
    sent = jnp.concatenate([dec_q.astype(jnp.bfloat16), dec_kv.astype(jnp.bfloat16), ids, pad], axis=1)
    got = tree_gather(sent)
    rows = tree_row(tok_place, owner_slots // dec_count, dec_count) + owner_slots % dec_count
    chosen = jnp.take(got, rows, axis=0)
    dec_query = chosen[:, :q_width]
    dec_keyval = chosen[:, q_width:q_width + 2 * kv_width].reshape(dec_count, 2, kv_width)
    served, new_pool = serve_owner(dec_query, dec_keyval, dec_lengths, dec_pool)
    back = tree_gather(served)
    got_ids = got[:, q_width + 2 * kv_width:used].astype(jnp.int32)
    requests = got_ids[:, 0] * dec_count + got_ids[:, 1]
    wanted = tok_place * dec_count + jnp.arange(dec_count, dtype=jnp.int32)
    where = jnp.argmax(requests[None, :] == wanted[:, None], axis=1)
    dec_attn = jnp.take(back, where, axis=0)
    all_query, all_keyval = pre_q, pre_kv
    return dec_attn, new_pool, all_query, all_keyval


def prefill(all_query, all_keyval, pre_tokens, w_query, w_keyval, pre_cache, pre_offsets):
    pre_count = pre_tokens.shape[0]
    q_width = w_query.shape[1]
    kv_width = w_keyval.shape[2]
    tok_place = lax.axis_index("tok")
    half_id = tok_place % 2
    offset = pre_offsets[tok_place // 2]
    local_pos = jnp.arange(pre_count, dtype=jnp.int32)
    positions = offset + half_id * pre_count + local_pos
    q_heads = q_width // HD
    kv_heads = kv_width // HD
    turned = rotate(all_query.reshape(pre_count, q_heads, HD), positions)
    turned = turned.astype(jnp.bfloat16).reshape(pre_count, q_width)
    pre_kv = all_keyval.reshape(pre_count, 2, kv_width)
    new_keys = rotate(pre_kv[:, 0].reshape(pre_count, kv_heads, HD), positions)
    new_keys = new_keys.astype(jnp.bfloat16).reshape(pre_count, kv_width)
    appended = jnp.stack([new_keys, pre_kv[:, 1].astype(jnp.bfloat16)], axis=0)
    shard = pre_cache.shape[1]
    other_cache, other_new = swapped((pre_cache, appended), "tok", 0)
    is_lower = half_id == 0
    history = jnp.where(
        is_lower,
        jnp.concatenate([pre_cache, other_cache], axis=1),
        jnp.concatenate([other_cache, pre_cache], axis=1),
    )
    block_rows = jnp.where(
        is_lower,
        jnp.concatenate([appended, other_new], axis=1),
        jnp.concatenate([other_new, appended], axis=1),
    )
    key_rows = jnp.concatenate([history, block_rows], axis=1)
    key_slots = jnp.arange(key_rows.shape[1], dtype=jnp.int32)
    key_pos = jnp.where(key_slots < 2 * shard, key_slots, offset + key_slots - 2 * shard)
    usable = (key_slots < offset) | (key_slots >= 2 * shard)
    key_pos = jnp.where(usable, key_pos, jnp.int32(1 << 30))
    return (turned, key_rows[0], key_rows[1], positions, key_pos), appended


def body(dec_tokens, pre_tokens, w_query, w_keyval, b_query, b_keyval, dec_pool, owner_slots, dec_lengths, pre_cache, pre_offsets):
    dec_attn, new_pool, all_query, all_keyval = body_inner(
        dec_tokens, pre_tokens, w_query, w_keyval, b_query, b_keyval, dec_pool, owner_slots, dec_lengths
    )
    operands, appended = prefill(all_query, all_keyval, pre_tokens, w_query, w_keyval, pre_cache, pre_offsets)
    pre_attn = attend(*operands)
    return (dec_attn, pre_attn, new_pool, appended)


def solution(mesh):
    in_specs = (
        P("tok", "kv"),
        P("tok", "kv"),
        P(None, "kv"),
        P(None, None, "kv"),
        P("kv"),
        P(None, "kv"),
        P(None, "tok", "kv"),
        P("tok"),
        P("tok"),
        P(None, "tok", "kv"),
        P(),
    )
    out_specs = (P("tok", "kv"), P("tok", "kv"), P(None, "tok", "kv"), P(None, "tok", "kv"))
    return jax.shard_map(body, mesh=mesh, in_specs=in_specs, out_specs=out_specs, check_vma=False)
```

```python
import jax
import jax.numpy as jnp
from jax import lax
from jax.sharding import PartitionSpec as P
from jax.experimental import pallas as pl

HD = 128


THETA = 1000000.0


def swapped(value, axis, distance):
    return lax.ppermute(value, axis, [(i, i ^ 1 << distance) for i in range(lax.axis_size(axis))])


def rotate(values, positions):
    halfway = values.shape[-1] // 2
    spread = jnp.arange(halfway, dtype=jnp.float32) * (2.0 / values.shape[-1])
    rates = jnp.power(jnp.float32(THETA), -spread)
    angles = positions.astype(jnp.float32)[:, None] * rates[None, :]
    cosine = jnp.cos(angles)[:, None, :]
    sine = jnp.sin(angles)[:, None, :]
    former = values[..., :halfway]
    latter = values[..., halfway:]
    return jnp.concatenate(
        [former * cosine - latter * sine, latter * cosine + former * sine], axis=-1
    )


def attend_kernel(q_ref, k_ref, v_ref, bias_ref, o_ref):
    scores = lax.dot_general(
        q_ref[...], k_ref[...], (((1,), (1,)), ((), ())), preferred_element_type=jnp.float32
    ) * HD ** (-0.5) + bias_ref[...]
    top = jnp.max(scores, axis=1, keepdims=True)
    powers = jnp.exp(scores - top)
    total = jnp.sum(powers, axis=1, keepdims=True)
    mixed = jnp.dot(powers.astype(jnp.bfloat16), v_ref[...], preferred_element_type=jnp.float32)
    o_ref[...] = (mixed / total).astype(o_ref.dtype)


def attend(queries, keys, values, bias):
    amount, width = queries.shape
    length = keys.shape[0]
    return pl.pallas_call(
        attend_kernel,
        grid=(width // HD,),
        in_specs=[
            pl.BlockSpec((amount, HD), lambda h: (0, h)),
            pl.BlockSpec((length, HD), lambda h: (0, 0)),
            pl.BlockSpec((length, HD), lambda h: (0, 0)),
            pl.BlockSpec((amount, length), lambda h: (0, 0)),
        ],
        out_specs=pl.BlockSpec((amount, HD), lambda h: (0, h)),
        out_shape=jax.ShapeDtypeStruct((amount, width), jnp.bfloat16),
    )(queries, keys, values, bias)


def head_scores(queries, key_rows, allowed):
    amount = queries.shape[0]
    q_heads = queries.shape[1] // HD
    shaped = queries.reshape(amount, q_heads, HD)
    product = jnp.einsum("ngd,md->ngm", shaped, key_rows, preferred_element_type=jnp.float32)
    scores = product * HD ** (-0.5)
    return jnp.where(allowed[:, None, :], scores, -jnp.inf)


def head_mix(scores, peaks, value_rows):
    powers = jnp.exp(scores - peaks[..., None])
    totals = jnp.sum(powers, axis=-1)
    weights = powers.astype(jnp.bfloat16)
    product = jnp.einsum("ngm,md->ngd", weights, value_rows, preferred_element_type=jnp.float32)
    return (totals, product)


def serve_owner(queries, keyval, lengths, cache_pool):
    amount = queries.shape[0]
    q_heads = queries.shape[1] // HD
    kv_heads = cache_pool.shape[2] // HD
    finish = jnp.cumsum(lengths + 1)
    starts = finish - lengths - 1
    turned = rotate(queries.astype(jnp.float32).reshape(amount, q_heads, HD), lengths)
    turned = turned.astype(jnp.bfloat16).reshape(amount, q_heads * HD)
    new_keys = rotate(keyval[:, 0].astype(jnp.float32).reshape(amount, kv_heads, HD), lengths)
    new_keys = new_keys.astype(jnp.bfloat16).reshape(amount, kv_heads * HD)
    appended = jnp.stack([new_keys, keyval[:, 1]], axis=0)
    cache_pool = cache_pool.at[:, starts + lengths].set(appended)
    spots = jnp.arange(cache_pool.shape[1], dtype=jnp.int32)
    allowed = (spots[None, :] >= starts[:, None]) & (spots[None, :] <= (starts + lengths)[:, None])
    scores = head_scores(turned, cache_pool[0], allowed)
    totals, mixed = head_mix(scores, jnp.max(scores, axis=-1), cache_pool[1])
    result = (mixed / totals[..., None]).astype(jnp.bfloat16).reshape(amount, q_heads * HD)
    return (result, cache_pool)


def tree_gather(value):
    buffer = value
    for stride, count in ((1, 2), (2, 4), (8, 4)):
      parts = [buffer]
      for shift in range(1, count):
          pairs = []
          for i in range(32):
              digit = (i // stride) % count
              target = i + (((digit + shift) % count) - digit) * stride
              pairs.append((i, target))
          parts.append(lax.ppermute(buffer, "tok", pairs))
      buffer = jnp.concatenate(parts, axis=0)
    return buffer


def tree_row(place, source, rows):
    core = (place % 2) ^ (source % 2)
    y = ((place // 2) % 4 - (source // 2) % 4) % 4
    z = (place // 8 - source // 8) % 4
    return ((z * 4 + y) * 2 + core) * rows


def swap_columns(rows):
    count = lax.axis_size("kv")
    tiled = jnp.broadcast_to(rows[None], (count,) + rows.shape)
    blocks = lax.all_to_all(tiled, "kv", 0, 0, tiled=False)
    return jnp.transpose(blocks, (1, 0, 2)).reshape(rows.shape[0], count * rows.shape[1])


def block_project(rows, after, w_query, kv_weight, b_query, kv_bias):
    count = lax.axis_size("kv")
    width = rows.shape[1]
    tiled = jnp.broadcast_to(rows[None], (count,) + rows.shape)
    tiled, after = lax.optimization_barrier((tiled, after))
    blocks = lax.all_to_all(tiled, "kv", 0, 0, tiled=False)
    cols = jnp.transpose(blocks, (1, 0, 2)).reshape(rows.shape[0], count * width)
    query = jnp.dot(cols, w_query, preferred_element_type=jnp.float32) + b_query
    keyval = jnp.dot(cols, kv_weight, preferred_element_type=jnp.float32) + kv_bias
    return query, keyval, after


def body_inner(dec_tokens, pre_tokens, w_query, w_keyval, b_query, b_keyval, dec_pool, owner_slots, dec_lengths):
    dec_count = dec_tokens.shape[0]
    q_width = w_query.shape[1]
    kv_width = w_keyval.shape[2]
    kv_weight = w_keyval.reshape(w_keyval.shape[0], 2 * kv_width)
    kv_bias = b_keyval.reshape(2 * kv_width)
    dec_cols = swap_columns(dec_tokens)
    pre_q, pre_kv, dec_cols = block_project(pre_tokens, dec_cols, w_query, kv_weight, b_query, kv_bias)
    dec_q = jnp.dot(dec_cols, w_query, preferred_element_type=jnp.float32) + b_query
    dec_kv = jnp.dot(dec_cols, kv_weight, preferred_element_type=jnp.float32) + kv_bias
    tok_place = lax.axis_index("tok")
    ids = jnp.stack([owner_slots // dec_count, owner_slots % dec_count], axis=1).astype(jnp.bfloat16)
    used = q_width + 2 * kv_width + 2
    pad = jnp.zeros((dec_count, -(-used // 128) * 128 - used), jnp.bfloat16)
    sent = jnp.concatenate([dec_q.astype(jnp.bfloat16), dec_kv.astype(jnp.bfloat16), ids, pad], axis=1)
    got = tree_gather(sent)
    rows = tree_row(tok_place, owner_slots // dec_count, dec_count) + owner_slots % dec_count
    chosen = jnp.take(got, rows, axis=0)
    dec_query = chosen[:, :q_width]
    dec_keyval = chosen[:, q_width:q_width + 2 * kv_width].reshape(dec_count, 2, kv_width)
    served, new_pool = serve_owner(dec_query, dec_keyval, dec_lengths, dec_pool)
    back = tree_gather(served)
    got_ids = got[:, q_width + 2 * kv_width:used].astype(jnp.int32)
    requests = got_ids[:, 0] * dec_count + got_ids[:, 1]
    wanted = tok_place * dec_count + jnp.arange(dec_count, dtype=jnp.int32)
    where = jnp.argmax(requests[None, :] == wanted[:, None], axis=1)
    dec_attn = jnp.take(back, where, axis=0)
    all_query, all_keyval = pre_q, pre_kv
    return dec_attn, new_pool, all_query, all_keyval


def prefill(all_query, all_keyval, pre_tokens, w_query, w_keyval, pre_cache, pre_offsets):
    pre_count = pre_tokens.shape[0]
    q_width = w_query.shape[1]
    kv_width = w_keyval.shape[2]
    tok_place = lax.axis_index("tok")
    half_id = tok_place % 2
    offset = pre_offsets[tok_place // 2]
    local_pos = jnp.arange(pre_count, dtype=jnp.int32)
    positions = offset + half_id * pre_count + local_pos
    q_heads = q_width // HD
    kv_heads = kv_width // HD
    turned = rotate(all_query.reshape(pre_count, q_heads, HD), positions)
    turned = turned.astype(jnp.bfloat16).reshape(pre_count, q_width)
    pre_kv = all_keyval.reshape(pre_count, 2, kv_width)
    new_keys = rotate(pre_kv[:, 0].reshape(pre_count, kv_heads, HD), positions)
    new_keys = new_keys.astype(jnp.bfloat16).reshape(pre_count, kv_width)
    appended = jnp.stack([new_keys, pre_kv[:, 1].astype(jnp.bfloat16)], axis=0)
    shard = pre_cache.shape[1]
    other_cache, other_new = swapped((pre_cache, appended), "tok", 0)
    is_lower = half_id == 0
    history = jnp.where(
        is_lower,
        jnp.concatenate([pre_cache, other_cache], axis=1),
        jnp.concatenate([other_cache, pre_cache], axis=1),
    )
    block_rows = jnp.where(
        is_lower,
        jnp.concatenate([appended, other_new], axis=1),
        jnp.concatenate([other_new, appended], axis=1),
    )
    key_rows = jnp.concatenate([history, block_rows], axis=1)
    key_slots = jnp.arange(key_rows.shape[1], dtype=jnp.int32)
    key_pos = jnp.where(key_slots < 2 * shard, key_slots, offset + key_slots - 2 * shard)
    usable = (key_slots < offset) | (key_slots >= 2 * shard)
    key_pos = jnp.where(usable, key_pos, jnp.int32(1 << 30))
    bias = jnp.where(key_pos[None, :] <= positions[:, None], jnp.float32(0), -jnp.inf)
    return (turned, key_rows[0], key_rows[1], bias), appended


def body(dec_tokens, pre_tokens, w_query, w_keyval, b_query, b_keyval, dec_pool, owner_slots, dec_lengths, pre_cache, pre_offsets):
    dec_attn, new_pool, all_query, all_keyval = body_inner(
        dec_tokens, pre_tokens, w_query, w_keyval, b_query, b_keyval, dec_pool, owner_slots, dec_lengths
    )
    operands, appended = prefill(all_query, all_keyval, pre_tokens, w_query, w_keyval, pre_cache, pre_offsets)
    pre_attn = attend(*operands)
    return (dec_attn, pre_attn, new_pool, appended)


def solution(mesh):
    in_specs = (
        P("tok", "kv"),
        P("tok", "kv"),
        P(None, "kv"),
        P(None, None, "kv"),
        P("kv"),
        P(None, "kv"),
        P(None, "tok", "kv"),
        P("tok"),
        P("tok"),
        P(None, "tok", "kv"),
        P(),
    )
    out_specs = (P("tok", "kv"), P("tok", "kv"), P(None, "tok", "kv"), P(None, "tok", "kv"))
    return jax.shard_map(body, mesh=mesh, in_specs=in_specs, out_specs=out_specs, check_vma=False)
```

```python
import jax
import jax.numpy as jnp
from jax import lax
from jax.sharding import PartitionSpec as P
from jax.experimental import pallas as pl

HD = 128


THETA = 1000000.0


def swapped(value, axis, distance):
    return lax.ppermute(value, axis, [(i, i ^ 1 << distance) for i in range(lax.axis_size(axis))])


def rotate(values, positions):
    halfway = values.shape[-1] // 2
    spread = jnp.arange(halfway, dtype=jnp.float32) * (2.0 / values.shape[-1])
    rates = jnp.power(jnp.float32(THETA), -spread)
    angles = positions.astype(jnp.float32)[:, None] * rates[None, :]
    cosine = jnp.cos(angles)[:, None, :]
    sine = jnp.sin(angles)[:, None, :]
    former = values[..., :halfway]
    latter = values[..., halfway:]
    return jnp.concatenate(
        [former * cosine - latter * sine, latter * cosine + former * sine], axis=-1
    )


def attend_kernel(q_ref, k_ref, v_ref, qpos_ref, kpos_ref, o_ref):
    scores = lax.dot_general(
        q_ref[...], k_ref[...], (((1,), (1,)), ((), ())), preferred_element_type=jnp.float32
    ) * HD ** (-0.5)
    allowed = kpos_ref[...] <= qpos_ref[...]
    scores = jnp.where(allowed, scores, -jnp.inf)
    top = jnp.max(scores, axis=1, keepdims=True)
    powers = jnp.exp(scores - top)
    total = jnp.sum(powers, axis=1, keepdims=True)
    mixed = jnp.dot(powers.astype(jnp.bfloat16), v_ref[...], preferred_element_type=jnp.float32)
    o_ref[...] = (mixed / total).astype(o_ref.dtype)


def attend(queries, keys, values, query_pos, key_pos):
    amount, width = queries.shape
    length = keys.shape[0]
    return pl.pallas_call(
        attend_kernel,
        grid=(width // HD,),
        in_specs=[
            pl.BlockSpec((amount, HD), lambda h: (0, h)),
            pl.BlockSpec((length, HD), lambda h: (0, 0)),
            pl.BlockSpec((length, HD), lambda h: (0, 0)),
            pl.BlockSpec((amount, 1), lambda h: (0, 0)),
            pl.BlockSpec((1, length), lambda h: (0, 0)),
        ],
        out_specs=pl.BlockSpec((amount, HD), lambda h: (0, h)),
        out_shape=jax.ShapeDtypeStruct((amount, width), jnp.bfloat16),
    )(queries, keys, values, query_pos.reshape(amount, 1), key_pos.reshape(1, length))


def head_scores(queries, key_rows, allowed):
    amount = queries.shape[0]
    q_heads = queries.shape[1] // HD
    shaped = queries.reshape(amount, q_heads, HD)
    product = jnp.einsum("ngd,md->ngm", shaped, key_rows, preferred_element_type=jnp.float32)
    scores = product * HD ** (-0.5)
    return jnp.where(allowed[:, None, :], scores, -jnp.inf)


def head_mix(scores, peaks, value_rows):
    powers = jnp.exp(scores - peaks[..., None])
    totals = jnp.sum(powers, axis=-1)
    weights = powers.astype(jnp.bfloat16)
    product = jnp.einsum("ngm,md->ngd", weights, value_rows, preferred_element_type=jnp.float32)
    return (totals, product)


def serve_owner(queries, keyval, lengths, cache_pool):
    amount = queries.shape[0]
    q_heads = queries.shape[1] // HD
    kv_heads = cache_pool.shape[2] // HD
    finish = jnp.cumsum(lengths + 1)
    starts = finish - lengths - 1
    turned = rotate(queries.astype(jnp.float32).reshape(amount, q_heads, HD), lengths)
    turned = turned.astype(jnp.bfloat16).reshape(amount, q_heads * HD)
    new_keys = rotate(keyval[:, 0].astype(jnp.float32).reshape(amount, kv_heads, HD), lengths)
    new_keys = new_keys.astype(jnp.bfloat16).reshape(amount, kv_heads * HD)
    appended = jnp.stack([new_keys, keyval[:, 1]], axis=0)
    cache_pool = cache_pool.at[:, starts + lengths].set(appended)
    spots = jnp.arange(cache_pool.shape[1], dtype=jnp.int32)
    allowed = (spots[None, :] >= starts[:, None]) & (spots[None, :] <= (starts + lengths)[:, None])
    scores = head_scores(turned, cache_pool[0], allowed)
    totals, mixed = head_mix(scores, jnp.max(scores, axis=-1), cache_pool[1])
    result = (mixed / totals[..., None]).astype(jnp.bfloat16).reshape(amount, q_heads * HD)
    return (result, cache_pool)


def tree_gather(value):
    buffer = value
    for level, stride, count in (("c", 1, 2), ("y", 2, 4), ("z", 8, 4)):
      parts = [buffer]
      for shift in range(1, count):
          pairs = []
          for i in range(32):
              digit = (i // stride) % count
              target = i + (((digit + shift) % count) - digit) * stride
              pairs.append((i, target))
          parts.append(lax.ppermute(buffer, "tok", pairs))
      if level != "z":
          buffer = jnp.concatenate(parts, axis=0)
    return parts


def pick(parts, rows):
    block = parts[0].shape[0]
    out = None
    for k, part in enumerate(parts):
        onehot = (rows[:, None] == k * block + jnp.arange(block, dtype=jnp.int32)[None, :]).astype(part.dtype)
        piece = jnp.dot(onehot, part, preferred_element_type=jnp.float32)
        out = piece if out is None else out + piece
    return out.astype(parts[0].dtype)


def tree_row(place, source, rows):
    core = (place % 2) ^ (source % 2)
    y = ((place // 2) % 4 - (source // 2) % 4) % 4
    z = (place // 8 - source // 8) % 4
    return ((z * 4 + y) * 2 + core) * rows


def swap_columns(rows):
    count = lax.axis_size("kv")
    tiled = jnp.broadcast_to(rows[None], (count,) + rows.shape)
    blocks = lax.all_to_all(tiled, "kv", 0, 0, tiled=False)
    return jnp.transpose(blocks, (1, 0, 2)).reshape(rows.shape[0], count * rows.shape[1])


def block_project(rows, after, w_query, kv_weight, b_query, kv_bias):
    count = lax.axis_size("kv")
    width = rows.shape[1]
    tiled = jnp.broadcast_to(rows[None], (count,) + rows.shape)
    tiled, after = lax.optimization_barrier((tiled, after))
    blocks = lax.all_to_all(tiled, "kv", 0, 0, tiled=False)
    cols = jnp.transpose(blocks, (1, 0, 2)).reshape(rows.shape[0], count * width)
    query = jnp.dot(cols, w_query, preferred_element_type=jnp.float32) + b_query
    keyval = jnp.dot(cols, kv_weight, preferred_element_type=jnp.float32) + kv_bias
    return query, keyval, after


def body_inner(dec_tokens, pre_tokens, w_query, w_keyval, b_query, b_keyval, dec_pool, owner_slots, dec_lengths):
    dec_count = dec_tokens.shape[0]
    q_width = w_query.shape[1]
    kv_width = w_keyval.shape[2]
    kv_weight = w_keyval.reshape(w_keyval.shape[0], 2 * kv_width)
    kv_bias = b_keyval.reshape(2 * kv_width)
    dec_cols = swap_columns(dec_tokens)
    pre_q, pre_kv, dec_cols = block_project(pre_tokens, dec_cols, w_query, kv_weight, b_query, kv_bias)
    dec_q = jnp.dot(dec_cols, w_query, preferred_element_type=jnp.float32) + b_query
    dec_kv = jnp.dot(dec_cols, kv_weight, preferred_element_type=jnp.float32) + kv_bias
    tok_place = lax.axis_index("tok")
    ids = jnp.stack([owner_slots // dec_count, owner_slots % dec_count], axis=1).astype(jnp.bfloat16)
    used = q_width + 2 * kv_width + 2
    pad = jnp.zeros((dec_count, -(-used // 128) * 128 - used), jnp.bfloat16)
    sent = jnp.concatenate([dec_q.astype(jnp.bfloat16), dec_kv.astype(jnp.bfloat16), ids, pad], axis=1)
    got = tree_gather(sent)
    rows = tree_row(tok_place, owner_slots // dec_count, dec_count) + owner_slots % dec_count
    chosen = pick(got, rows)
    dec_query = chosen[:, :q_width]
    dec_keyval = chosen[:, q_width:q_width + 2 * kv_width].reshape(dec_count, 2, kv_width)
    served, new_pool = serve_owner(dec_query, dec_keyval, dec_lengths, dec_pool)
    back = tree_gather(served)
    got_ids = jnp.concatenate([part[:, q_width + 2 * kv_width:used] for part in got], axis=0).astype(jnp.int32)
    requests = got_ids[:, 0] * dec_count + got_ids[:, 1]
    wanted = tok_place * dec_count + jnp.arange(dec_count, dtype=jnp.int32)
    where = jnp.argmax(requests[None, :] == wanted[:, None], axis=1)
    dec_attn = pick(back, where.astype(jnp.int32))
    all_query, all_keyval = pre_q, pre_kv
    return dec_attn, new_pool, all_query, all_keyval


def prefill(all_query, all_keyval, pre_tokens, w_query, w_keyval, pre_cache, pre_offsets):
    pre_count = pre_tokens.shape[0]
    q_width = w_query.shape[1]
    kv_width = w_keyval.shape[2]
    tok_place = lax.axis_index("tok")
    half_id = tok_place % 2
    offset = pre_offsets[tok_place // 2]
    local_pos = jnp.arange(pre_count, dtype=jnp.int32)
    positions = offset + half_id * pre_count + local_pos
    q_heads = q_width // HD
    kv_heads = kv_width // HD
    turned = rotate(all_query.reshape(pre_count, q_heads, HD), positions)
    turned = turned.astype(jnp.bfloat16).reshape(pre_count, q_width)
    pre_kv = all_keyval.reshape(pre_count, 2, kv_width)
    new_keys = rotate(pre_kv[:, 0].reshape(pre_count, kv_heads, HD), positions)
    new_keys = new_keys.astype(jnp.bfloat16).reshape(pre_count, kv_width)
    appended = jnp.stack([new_keys, pre_kv[:, 1].astype(jnp.bfloat16)], axis=0)
    shard = pre_cache.shape[1]
    other_cache, other_new = swapped((pre_cache, appended), "tok", 0)
    is_lower = half_id == 0
    history = jnp.where(
        is_lower,
        jnp.concatenate([pre_cache, other_cache], axis=1),
        jnp.concatenate([other_cache, pre_cache], axis=1),
    )
    block_rows = jnp.where(
        is_lower,
        jnp.concatenate([appended, other_new], axis=1),
        jnp.concatenate([other_new, appended], axis=1),
    )
    key_rows = jnp.concatenate([history, block_rows], axis=1)
    key_slots = jnp.arange(key_rows.shape[1], dtype=jnp.int32)
    key_pos = jnp.where(key_slots < 2 * shard, key_slots, offset + key_slots - 2 * shard)
    usable = (key_slots < offset) | (key_slots >= 2 * shard)
    key_pos = jnp.where(usable, key_pos, jnp.int32(1 << 30))
    return (turned, key_rows[0], key_rows[1], positions, key_pos), appended


def body(dec_tokens, pre_tokens, w_query, w_keyval, b_query, b_keyval, dec_pool, owner_slots, dec_lengths, pre_cache, pre_offsets):
    dec_attn, new_pool, all_query, all_keyval = body_inner(
        dec_tokens, pre_tokens, w_query, w_keyval, b_query, b_keyval, dec_pool, owner_slots, dec_lengths
    )
    operands, appended = prefill(all_query, all_keyval, pre_tokens, w_query, w_keyval, pre_cache, pre_offsets)
    pre_attn = attend(*operands)
    return (dec_attn, pre_attn, new_pool, appended)


def solution(mesh):
    in_specs = (
        P("tok", "kv"),
        P("tok", "kv"),
        P(None, "kv"),
        P(None, None, "kv"),
        P("kv"),
        P(None, "kv"),
        P(None, "tok", "kv"),
        P("tok"),
        P("tok"),
        P(None, "tok", "kv"),
        P(),
    )
    out_specs = (P("tok", "kv"), P("tok", "kv"), P(None, "tok", "kv"), P(None, "tok", "kv"))
    return jax.shard_map(body, mesh=mesh, in_specs=in_specs, out_specs=out_specs, check_vma=False)
```
